256 devices in a mesh: section: 4 (over x), seq: 16 (over z, y_hi), tp: 4 (over y_lo, core).
Axes of the slice: x: 4, y: 4 (y_hi: 2, y_lo: 2; y = y_hi * 2 + y_lo), z: 8, core: 2. Of those that a mesh axis runs over, the one named last changes fastest.
Arguments:
- queries: bfloat16 [4, 4096, 8192], P('section', 'seq', 'tp'), may hold values from -135 to 135
- upstream: bfloat16 [4, 4096, 8192], P('section', 'seq', 'tp'), may hold values from -48 to 48
- shared_kv: bfloat16 [2, 4096, 1024], P(None, ('seq', 'tp')), may hold values from -5 to 5
Outputs:
- d_queries: bfloat16 [4, 4096, 8192], P('section', 'seq', 'tp')
- d_shared_kv: float32 [2, 4096, 1024], P(None, ('seq', 'tp'))
The draws below stay inside these ranges and needn't reach their ends.
All inputs are finite; a program needn't handle non-finite values.
Results may differ from the reference program's by a relative error of at most 0.0098.
Values may be sent and summed in bfloat16 or wider, within the bound.
No kernel may reach another device: no remote copies, remote signals or barrier semaphores. Data moves between devices by JAX's collectives and lax.ppermute only.
A program may use at most 128 MiB of HBM per device.

```python
import math
import jax
import jax.numpy as jnp
from jax import lax

QH = 64
KVH = 8
HD = 128
WINDOW = 1024
TOK_DEV = 256
LAYERS = 4
TOKENS = 4096
QD = 8192
KVD = 1024


def kv_tables(key):
    base_key = jax.random.fold_in(key, 17)
    first_key, second_key = jax.random.split(base_key)
    keys_table = jnp.clip(jax.random.normal(first_key, (TOKENS, KVD), jnp.float32), -5.0, 5.0)
    value_table = jnp.clip(jax.random.normal(second_key, (TOKENS, KVD), jnp.float32), -5.0, 5.0)
    return (keys_table, value_table)


def draw_shared_kv(key, part):
    keys_table, value_table = kv_tables(key)
    return jnp.stack([keys_table, value_table]).astype(jnp.bfloat16)


def draw_queries(key, part):
    drawn = jnp.clip(jax.random.normal(jax.random.fold_in(key, 29), (LAYERS, TOKENS, QD), jnp.float32), -5.0, 5.0)
    return drawn.astype(jnp.bfloat16)


def level_of(own_key, extent, cuts, least, top_value):
    level, own = 1.0, jax.random.fold_in(own_key, 6)
    for dim, shards_of in cuts:
        steps = jnp.exp(jax.random.uniform(jax.random.fold_in(own, dim), (shards_of,), jnp.float32, least / len(cuts), top_value / len(cuts)))
        level = level * jnp.repeat(steps, extent[dim] // shards_of).reshape([-1 if axis == dim else 1 for axis in range(len(extent))])
    return level


def noise(rng, extent, width, reach, pieces=(), kind=jnp.bfloat16):
    loudness = level_of(rng, extent, pieces, -0.22, 0.18) if pieces else 1.0
    values = jax.random.normal(rng, extent, jnp.float32) * width * loudness
    return jnp.minimum(jnp.maximum(values, -reach), reach).astype(kind)


def setup_inputs(seed: int = 0) -> dict:
    key_of = jax.random.split(jax.random.key(seed), 4)
    return {
        "queries": draw_queries(jax.random.fold_in(key_of[3], 71), 0),
        "upstream": noise(key_of[1], (LAYERS, TOKENS, QD), 8.0, 48.0, ((0, 4), (1, 16), (2, 4))),
        "shared_kv": draw_shared_kv(jax.random.fold_in(key_of[3], 71), 0),
    }


def block_grads(query_block, grad_block, kv_window, allowed, score_scale):
    query_wide = query_block.astype(jnp.float32)
    keys_wide = kv_window[0].astype(jnp.float32)
    values_wide = kv_window[1].astype(jnp.float32)
    grad_wide = grad_block.astype(jnp.float32)
    scores = jnp.einsum('rkgd,ekd->kgre', query_wide, keys_wide) * score_scale
    masked = jnp.where(allowed, scores, -jnp.inf)
    highest = lax.optimization_barrier(jnp.max(masked, axis=-1, keepdims=True))
    weights = jnp.exp(masked - highest)
    probs = weights / lax.optimization_barrier(jnp.sum(weights, axis=-1, keepdims=True))
    probs_b = lax.optimization_barrier(probs.astype(jnp.bfloat16))
    probs_wide = probs_b.astype(jnp.float32)
    attn_out = jnp.einsum('kgre,ekd->rkgd', probs_wide, values_wide)
    delta = lax.optimization_barrier(jnp.sum(grad_wide * attn_out, axis=-1))
    dprobs = jnp.einsum('rkgd,ekd->kgre', grad_wide, values_wide)
    dscores = probs * (dprobs - jnp.transpose(delta, (1, 2, 0))[..., None])
    dscores_b = lax.optimization_barrier(dscores.astype(jnp.bfloat16))
    dscores_wide = dscores_b.astype(jnp.float32)
    grad_query = jnp.einsum('kgre,ekd->rkgd', dscores_wide, keys_wide) * score_scale
    grad_key = jnp.einsum('kgre,rkgd->ekd', dscores_wide, query_wide) * score_scale
    grad_value = jnp.einsum('kgre,rkgd->ekd', probs_wide, grad_wide)
    return (grad_query, grad_key, grad_value)

def reference(queries, upstream, shared_kv):
    score_scale = 1.0 / math.sqrt(HD)
    group_size = QH // KVH
    padded = jnp.pad(shared_kv, ((0, 0), (WINDOW, 0), (0, 0)))
    block_count = TOKENS // TOK_DEV
    ext_rows = WINDOW + TOK_DEV
    row_ids = lax.broadcasted_iota(jnp.int32, (TOK_DEV, ext_rows), 0)
    key_ids = lax.broadcasted_iota(jnp.int32, (TOK_DEV, ext_rows), 1)
    banded = (key_ids >= row_ids + 1) & (key_ids <= row_ids + WINDOW)
    totals = jnp.zeros((2, WINDOW + TOKENS, KVD), jnp.float32)
    layer_grads = []
    for layer_index in range(LAYERS):
        layer_queries = queries[layer_index]
        layer_upstream = upstream[layer_index]

        def advance(carried, block_index):
            first_row = (block_index * TOK_DEV).astype(jnp.int32)
            kv_window = lax.dynamic_slice_in_dim(padded, first_row, ext_rows, 1).reshape(2, ext_rows, KVH, HD)
            query_block = lax.dynamic_slice_in_dim(layer_queries, first_row, TOK_DEV, 0).reshape(TOK_DEV, KVH, group_size, HD)
            grad_block = lax.dynamic_slice_in_dim(layer_upstream, first_row, TOK_DEV, 0).reshape(TOK_DEV, KVH, group_size, HD)
            allowed = banded & (first_row - WINDOW + key_ids >= 0)
            grad_query, grad_key, grad_value = block_grads(query_block, grad_block, kv_window, allowed, score_scale)
            addition = jnp.stack([grad_key, grad_value]).reshape(2, ext_rows, KVD)
            previous = lax.dynamic_slice_in_dim(carried, first_row, ext_rows, 1)
            carried = lax.dynamic_update_slice_in_dim(carried, previous + addition, first_row, 1)
            return (carried, grad_query.reshape(TOK_DEV, QD).astype(jnp.bfloat16))
        totals, grad_rows = lax.scan(advance, totals, jnp.arange(block_count, dtype=jnp.int32))
        layer_grads.append(grad_rows.reshape(TOKENS, QD))
    return (jnp.stack(layer_grads), totals[:, WINDOW:, :])
```

```python
import math

import jax
import jax.numpy as jnp
from jax import lax
from jax.sharding import PartitionSpec as P

QH = 64
KVH = 8
HD = 128
WINDOW = 1024


def shifted(value, axis, by):
    peers = lax.axis_size(axis)
    pairs = [(i, i + by) for i in range(peers) if 0 <= i + by < peers]
    return lax.ppermute(value, axis, pairs)


def head_grads(query_block, grad_block, keys_head, values_head, allowed, score_scale):
    scores = (
        jnp.einsum("rgd,ed->gre", query_block, keys_head, preferred_element_type=jnp.float32)
        * score_scale
    )
    masked = jnp.where(allowed[None], scores, -jnp.inf)
    highest = jnp.max(masked, axis=-1, keepdims=True)
    weights = jnp.exp(masked - highest)
    probs = weights / jnp.sum(weights, axis=-1, keepdims=True)
    probs_b = probs.astype(jnp.bfloat16)
    attn_out = jnp.einsum("gre,ed->rgd", probs_b, values_head, preferred_element_type=jnp.float32)
    delta = jnp.sum(grad_block.astype(jnp.float32) * attn_out, axis=-1)
    dprobs = jnp.einsum("rgd,ed->gre", grad_block, values_head, preferred_element_type=jnp.float32)
    dscores = probs * (dprobs - jnp.transpose(delta)[:, :, None])
    dscores_b = dscores.astype(jnp.bfloat16)
    grad_query = (
        jnp.einsum("gre,ed->rgd", dscores_b, keys_head, preferred_element_type=jnp.float32)
        * score_scale
    )
    grad_key = (
        jnp.einsum("gre,rgd->ed", dscores_b, query_block, preferred_element_type=jnp.float32)
        * score_scale
    )
    grad_value = jnp.einsum("gre,rgd->ed", probs_b, grad_block, preferred_element_type=jnp.float32)
    return (grad_query, grad_key, grad_value)


def body(queries, upstream, shared_kv):
    local_kv = lax.all_to_all(shared_kv, "tp", split_axis=2, concat_axis=1, tiled=True)
    tok_rows = local_kv.shape[1]
    kv_cols = local_kv.shape[2]
    head_size = HD
    local_kv_heads = kv_cols // head_size
    group_size = QH // KVH
    block_heads = max(1, group_size // 2)
    span_blocks = WINDOW // tok_rows
    score_scale = 1.0 / math.sqrt(head_size)
    earlier = [shifted(local_kv, "seq", span_blocks - offset) for offset in range(span_blocks)]
    extended = jnp.concatenate(earlier + [local_kv], axis=1)
    ext_rows = extended.shape[1]
    position = lax.axis_index("seq")
    row_ids = lax.broadcasted_iota(jnp.int32, (tok_rows, ext_rows), 0)
    key_ids = lax.broadcasted_iota(jnp.int32, (tok_rows, ext_rows), 1)
    allowed = (
        (key_ids >= row_ids + 1)
        & (key_ids <= row_ids + WINDOW)
        & (position * tok_rows - WINDOW + key_ids >= 0)
    )
    query_heads = queries.reshape(tok_rows, -1, head_size)
    grad_heads = upstream.reshape(tok_rows, -1, head_size)
    query_parts = []
    key_parts = []
    value_parts = []
    for kv_head in range(local_kv_heads):
        keys_head = extended[0, :, kv_head * head_size : (kv_head + 1) * head_size]
        values_head = extended[1, :, kv_head * head_size : (kv_head + 1) * head_size]
        key_total = jnp.zeros((ext_rows, head_size), jnp.float32)
        value_total = jnp.zeros((ext_rows, head_size), jnp.float32)
        for first_head in range(kv_head * group_size, (kv_head + 1) * group_size, block_heads):
            query_block = query_heads[:, first_head : first_head + block_heads]
            grad_block = grad_heads[:, first_head : first_head + block_heads]
            grad_query, grad_key, grad_value = head_grads(
                query_block, grad_block, keys_head, values_head, allowed, score_scale
            )
            query_parts.append(grad_query)
            key_total = key_total + grad_key
            value_total = value_total + grad_value
        key_parts.append(key_total)
        value_parts.append(value_total)
    d_queries = jnp.concatenate(query_parts, axis=1).reshape(1, tok_rows, -1).astype(jnp.bfloat16)
    grad_ext = jnp.stack([jnp.concatenate(key_parts, axis=1), jnp.concatenate(value_parts, axis=1)])
    own_rows = grad_ext[:, span_blocks * tok_rows :, :]
    for offset in range(span_blocks):
        own_rows = own_rows + shifted(
            grad_ext[:, offset * tok_rows : (offset + 1) * tok_rows, :].astype(jnp.bfloat16),
            "seq",
            offset - span_blocks,
        ).astype(jnp.float32)
    by_token = lax.all_to_all(own_rows, "tp", split_axis=1, concat_axis=2, tiled=True)
    sections = lax.axis_size("section")
    kinds, rows, cols = by_token.shape
    pieces = by_token.reshape(kinds, sections, rows // sections, cols)
    pieces = lax.all_to_all(pieces, "section", split_axis=1, concat_axis=1)
    chunk = pieces[:, 0]
    for other in range(1, sections):
        chunk = chunk + pieces[:, other]
    d_shared_kv = lax.all_gather(chunk, "section", axis=1, tiled=True)
    return (d_queries, d_shared_kv)


def solution(mesh):
    in_specs = (P("section", "seq", "tp"), P("section", "seq", "tp"), P(None, ("seq", "tp"), None))
    out_specs = (P("section", "seq", "tp"), P(None, ("seq", "tp"), None))
    return jax.shard_map(body, mesh=mesh, in_specs=in_specs, out_specs=out_specs, check_vma=False)
```

```python
import math

import jax
import jax.numpy as jnp
from jax import lax
from jax.sharding import PartitionSpec as P

QH = 64
KVH = 8
HD = 128
WINDOW = 1024


def shifted(value, axis, by):
    peers = lax.axis_size(axis)
    pairs = [(i, i + by) for i in range(peers) if 0 <= i + by < peers]
    return lax.ppermute(value, axis, pairs)


def head_grads(query_block, grad_block, keys_head, values_head, allowed, score_scale):
    scores = (
        jnp.einsum("rgd,ed->gre", query_block, keys_head, preferred_element_type=jnp.float32)
        * score_scale
    )
    masked = jnp.where(allowed[None], scores, -jnp.inf)
    highest = jnp.max(masked, axis=-1, keepdims=True)
    weights = jnp.exp(masked - highest)
    probs = weights / jnp.sum(weights, axis=-1, keepdims=True)
    probs_b = probs.astype(jnp.bfloat16)
    attn_out = jnp.einsum("gre,ed->rgd", probs_b, values_head, preferred_element_type=jnp.float32)
    delta = jnp.sum(grad_block.astype(jnp.float32) * attn_out, axis=-1)
    dprobs = jnp.einsum("rgd,ed->gre", grad_block, values_head, preferred_element_type=jnp.float32)
    dscores = probs * (dprobs - jnp.transpose(delta)[:, :, None])
    dscores_b = dscores.astype(jnp.bfloat16)
    grad_query = (
        jnp.einsum("gre,ed->rgd", dscores_b, keys_head, preferred_element_type=jnp.float32)
        * score_scale
    )
    grad_key = (
        jnp.einsum("gre,rgd->ed", dscores_b, query_block, preferred_element_type=jnp.float32)
        * score_scale
    )
    grad_value = jnp.einsum("gre,rgd->ed", probs_b, grad_block, preferred_element_type=jnp.float32)
    return (grad_query, grad_key, grad_value)


def send_back(grad_ext, span_blocks, tok_rows):
    own_rows = grad_ext[:, span_blocks * tok_rows :, :]
    for offset in range(span_blocks):
        own_rows = own_rows + shifted(
            grad_ext[:, offset * tok_rows : (offset + 1) * tok_rows, :].astype(jnp.bfloat16),
            "seq",
            offset - span_blocks,
        ).astype(jnp.float32)
    return own_rows


def scatter_layers(own_rows):
    sections = lax.axis_size("section")
    peers = lax.axis_size("tp")
    kinds, rows, cols = own_rows.shape
    pieces = own_rows.reshape(kinds, peers, sections, rows // (peers * sections), cols)
    pieces = jnp.swapaxes(pieces, 1, 2).reshape(kinds, sections * peers, rows // (peers * sections), cols)
    pieces = lax.all_to_all(pieces, ("section", "tp"), split_axis=1, concat_axis=1)
    pieces = pieces.reshape(kinds, sections, peers, rows // (peers * sections), cols)
    chunk = pieces[:, 0]
    for other in range(1, sections):
        chunk = chunk + pieces[:, other]
    return jnp.swapaxes(chunk, 1, 2)


def body(queries, upstream, shared_kv):
    local_kv = lax.all_to_all(shared_kv, "tp", split_axis=2, concat_axis=1, tiled=True)
    tok_rows = local_kv.shape[1]
    kv_cols = local_kv.shape[2]
    head_size = HD
    local_kv_heads = kv_cols // head_size
    group_size = QH // KVH
    block_heads = max(1, group_size // 2)
    span_blocks = WINDOW // tok_rows
    score_scale = 1.0 / math.sqrt(head_size)
    position = lax.axis_index("seq")
    ext_rows = (span_blocks + 1) * tok_rows
    row_ids = lax.broadcasted_iota(jnp.int32, (tok_rows, ext_rows), 0)
    key_ids = lax.broadcasted_iota(jnp.int32, (tok_rows, ext_rows), 1)
    allowed = (
        (key_ids >= row_ids + 1)
        & (key_ids <= row_ids + WINDOW)
        & (position * tok_rows - WINDOW + key_ids >= 0)
    )
    query_heads = queries.reshape(tok_rows, -1, head_size)
    grad_heads = upstream.reshape(tok_rows, -1, head_size)
    arrived = []
    for kv_head in range(local_kv_heads):
        head_kv = local_kv[:, :, kv_head * head_size : (kv_head + 1) * head_size]
        earlier = [shifted(head_kv, "seq", span_blocks - offset) for offset in range(span_blocks)]
        arrived.append(jnp.concatenate(earlier + [head_kv], axis=1))
    query_parts = []
    chunks = []
    previous = None
    for kv_head in range(local_kv_heads):
        extended = arrived[kv_head]
        if previous is not None:
            extended, previous = lax.optimization_barrier((extended, previous))
            chunks.append(scatter_layers(send_back(previous, span_blocks, tok_rows)))
        keys_head = extended[0]
        values_head = extended[1]
        key_total = jnp.zeros((ext_rows, head_size), jnp.float32)
        value_total = jnp.zeros((ext_rows, head_size), jnp.float32)
        for first_head in range(kv_head * group_size, (kv_head + 1) * group_size, block_heads):
            query_block = query_heads[:, first_head : first_head + block_heads]
            grad_block = grad_heads[:, first_head : first_head + block_heads]
            grad_query, grad_key, grad_value = head_grads(
                query_block, grad_block, keys_head, values_head, allowed, score_scale
            )
            query_parts.append(grad_query)
            key_total = key_total + grad_key
            value_total = value_total + grad_value
        previous = jnp.stack([key_total, value_total])
    chunks.append(scatter_layers(send_back(previous, span_blocks, tok_rows)))
    d_queries = jnp.concatenate(query_parts, axis=1).reshape(1, tok_rows, -1).astype(jnp.bfloat16)
    kinds, rows, tp_peers, _ = chunks[0].shape
    joined = jnp.stack(chunks, axis=3).reshape(kinds, rows, -1)
    d_shared_kv = lax.all_gather(joined, "section", axis=1, tiled=True)
    return (d_queries, d_shared_kv)


def solution(mesh):
    in_specs = (P("section", "seq", "tp"), P("section", "seq", "tp"), P(None, ("seq", "tp"), None))
    out_specs = (P("section", "seq", "tp"), P(None, ("seq", "tp"), None))
    return jax.shard_map(body, mesh=mesh, in_specs=in_specs, out_specs=out_specs, check_vma=False)
```

```python
import functools
import math

import jax
import jax.numpy as jnp
from jax import lax
from jax.experimental import pallas as pl
from jax.experimental.pallas import tpu as pltpu
from jax.sharding import PartitionSpec as P

QH = 64
KVH = 8
HD = 128
WINDOW = 1024


def shifted(value, axis, by):
    peers = lax.axis_size(axis)
    pairs = [(i, i + by) for i in range(peers) if 0 <= i + by < peers]
    return lax.ppermute(value, axis, pairs)


def attn_kernel(mask_ref, q_ref, g_ref, k_ref, v_ref, dq_ref, dkv_ref, *, scale):
    gi = pl.program_id(1)
    q = q_ref[...]
    do = g_ref[...]
    k = k_ref[...]
    v = v_ref[...]
    nt = (((1,), (1,)), ((), ()))
    tn = (((0,), (0,)), ((), ()))
    s = lax.dot_general(q, k, nt, preferred_element_type=jnp.float32) * scale
    s = jnp.where(mask_ref[...] != 0, s, -jnp.inf)
    m = jnp.max(s, axis=1, keepdims=True)
    w = jnp.exp(s - m)
    p = w / jnp.sum(w, axis=1, keepdims=True)
    pb = p.astype(jnp.bfloat16)
    o = jnp.dot(pb, v, preferred_element_type=jnp.float32)
    delta = jnp.sum(do.astype(jnp.float32) * o, axis=1, keepdims=True)
    dp = lax.dot_general(do, v, nt, preferred_element_type=jnp.float32)
    dsb = (p * (dp - delta)).astype(jnp.bfloat16)
    dq = jnp.dot(dsb, k, preferred_element_type=jnp.float32) * scale
    dq_ref[...] = dq.astype(dq_ref.dtype)
    dk = lax.dot_general(dsb, q, tn, preferred_element_type=jnp.float32) * scale
    dv = lax.dot_general(pb, do, tn, preferred_element_type=jnp.float32)

    @pl.when(gi == 0)
    def _():
        dkv_ref[0] = dk
        dkv_ref[1] = dv

    @pl.when(gi > 0)
    def _():
        dkv_ref[0] += dk
        dkv_ref[1] += dv

def attention_grads(mask, q, g, ext, group, hd, scale):
    rows, qcols = q.shape
    _, ext_rows, kcols = ext.shape
    heads = kcols // hd
    flops = 6 * 2 * rows * ext_rows * hd * heads * group
    return pl.pallas_call(
        functools.partial(attn_kernel, scale=scale),
        grid=(heads, group),
        in_specs=[
            pl.BlockSpec((rows, ext_rows), lambda h, i: (0, 0)),
            pl.BlockSpec((rows, hd), lambda h, i: (0, h * group + i)),
            pl.BlockSpec((rows, hd), lambda h, i: (0, h * group + i)),
            pl.BlockSpec((None, ext_rows, hd), lambda h, i: (0, 0, h)),
            pl.BlockSpec((None, ext_rows, hd), lambda h, i: (1, 0, h)),
        ],
        out_specs=[
            pl.BlockSpec((rows, hd), lambda h, i: (0, h * group + i)),
            pl.BlockSpec((2, ext_rows, hd), lambda h, i: (0, 0, h)),
        ],
        out_shape=[
            jax.ShapeDtypeStruct((rows, qcols), jnp.bfloat16),
            jax.ShapeDtypeStruct((2, ext_rows, kcols), jnp.float32),
        ],
        compiler_params=pltpu.CompilerParams(dimension_semantics=("arbitrary", "arbitrary")),
        cost_estimate=pl.CostEstimate(flops=flops, transcendentals=rows * ext_rows * heads * group,
                                      bytes_accessed=2 * q.size * 2 + q.size * 2 + ext.size * 2 + ext.size * 4 + mask.size * 4),
    )(mask, q, g, ext, ext)


def scatter_layers(own_rows):
    sections = lax.axis_size("section")
    peers = lax.axis_size("tp")
    kinds, rows, cols = own_rows.shape
    pieces = own_rows.reshape(kinds, peers, sections, rows // (peers * sections), cols)
    pieces = jnp.swapaxes(pieces, 1, 2).reshape(kinds, sections * peers, rows // (peers * sections), cols)
    pieces = lax.all_to_all(pieces, ("section", "tp"), split_axis=1, concat_axis=1)
    pieces = pieces.reshape(kinds, sections, peers, rows // (peers * sections), cols)
    chunk = pieces[:, 0]
    for other in range(1, sections):
        chunk = chunk + pieces[:, other]
    return jnp.swapaxes(chunk, 1, 2)


def body(queries, upstream, shared_kv):
    local_kv = lax.all_to_all(shared_kv, "tp", split_axis=2, concat_axis=1, tiled=True)
    tok_rows = local_kv.shape[1]
    head_size = HD
    group_size = QH // KVH
    span_blocks = WINDOW // tok_rows
    score_scale = 1.0 / math.sqrt(head_size)
    earlier = [shifted(local_kv, "seq", span_blocks - offset) for offset in range(span_blocks)]
    extended = jnp.concatenate(earlier + [local_kv], axis=1)
    ext_rows = extended.shape[1]
    position = lax.axis_index("seq")
    row_ids = lax.broadcasted_iota(jnp.int32, (tok_rows, ext_rows), 0)
    key_ids = lax.broadcasted_iota(jnp.int32, (tok_rows, ext_rows), 1)
    allowed = (
        (key_ids >= row_ids + 1)
        & (key_ids <= row_ids + WINDOW)
        & (position * tok_rows - WINDOW + key_ids >= 0)
    )
    d_query_rows, grad_ext = attention_grads(
        allowed.astype(jnp.int32),
        queries.reshape(tok_rows, -1),
        upstream.reshape(tok_rows, -1),
        extended,
        group_size,
        head_size,
        score_scale,
    )
    d_queries = d_query_rows.reshape(queries.shape)
    own_rows = grad_ext[:, span_blocks * tok_rows :, :]
    for offset in range(span_blocks):
        own_rows = own_rows + shifted(
            grad_ext[:, offset * tok_rows : (offset + 1) * tok_rows, :].astype(jnp.bfloat16),
            "seq",
            offset - span_blocks,
        ).astype(jnp.float32)
    chunk = scatter_layers(own_rows)
    kinds, rows, tp_peers, cols = chunk.shape
    d_shared_kv = lax.all_gather(chunk.reshape(kinds, rows, -1), "section", axis=1, tiled=True)
    return (d_queries, d_shared_kv)


def solution(mesh):
    in_specs = (P("section", "seq", "tp"), P("section", "seq", "tp"), P(None, ("seq", "tp"), None))
    out_specs = (P("section", "seq", "tp"), P(None, ("seq", "tp"), None))
    return jax.shard_map(body, mesh=mesh, in_specs=in_specs, out_specs=out_specs, check_vma=False)
```

```python
import functools
import math

import jax
import jax.numpy as jnp
from jax import lax
from jax.experimental import pallas as pl
from jax.experimental.pallas import tpu as pltpu
from jax.sharding import PartitionSpec as P

QH = 64
KVH = 8
HD = 128
WINDOW = 1024


def shifted(value, axis, by):
    peers = lax.axis_size(axis)
    pairs = [(i, i + by) for i in range(peers) if 0 <= i + by < peers]
    return lax.ppermute(value, axis, pairs)


def attn_kernel(bias_ref, q_ref, g_ref, k_ref, v_ref, dq_ref, dkv_ref, *, scale, hd, per_step):
    gi = pl.program_id(1)
    k = k_ref[...]
    v = v_ref[...]
    bias = bias_ref[...]
    nt = (((1,), (1,)), ((), ()))
    tn = (((0,), (0,)), ((), ()))
    dk = None
    dv = None
    for part in range(per_step):
        cols = slice(part * hd, (part + 1) * hd)
        q = q_ref[:, cols]
        do = g_ref[:, cols]
        s = lax.dot_general(q, k, nt, preferred_element_type=jnp.float32) * scale + bias
        m = jnp.max(s, axis=1, keepdims=True)
        w = jnp.exp(s - m)
        p = w * (1.0 / jnp.sum(w, axis=1, keepdims=True))
        pb = p.astype(jnp.bfloat16)
        o = jnp.dot(pb, v, preferred_element_type=jnp.float32)
        delta = jnp.sum(do.astype(jnp.float32) * o, axis=1, keepdims=True)
        dp = lax.dot_general(do, v, nt, preferred_element_type=jnp.float32)
        dsb = (p * (dp - delta)).astype(jnp.bfloat16)
        dq = jnp.dot(dsb, k, preferred_element_type=jnp.float32) * scale
        dq_ref[:, cols] = dq.astype(dq_ref.dtype)
        dk_part = lax.dot_general(dsb, q, tn, preferred_element_type=jnp.float32) * scale
        dv_part = lax.dot_general(pb, do, tn, preferred_element_type=jnp.float32)
        dk = dk_part if dk is None else dk + dk_part
        dv = dv_part if dv is None else dv + dv_part

    @pl.when(gi == 0)
    def _():
        dkv_ref[0] = dk
        dkv_ref[1] = dv

    @pl.when(gi > 0)
    def _():
        dkv_ref[0] += dk
        dkv_ref[1] += dv


def attention_grads(bias, q, g, ext, group, hd, scale, per_step):
    rows, qcols = q.shape
    _, ext_rows, kcols = ext.shape
    heads = kcols // hd
    steps = group // per_step
    width = per_step * hd
    flops = 6 * 2 * rows * ext_rows * hd * heads * group
    return pl.pallas_call(
        functools.partial(attn_kernel, scale=scale, hd=hd, per_step=per_step),
        grid=(heads, steps),
        in_specs=[
            pl.BlockSpec((rows, ext_rows), lambda h, i: (0, 0)),
            pl.BlockSpec((rows, width), lambda h, i: (0, h * steps + i)),
            pl.BlockSpec((rows, width), lambda h, i: (0, h * steps + i)),
            pl.BlockSpec((None, ext_rows, hd), lambda h, i: (0, 0, h)),
            pl.BlockSpec((None, ext_rows, hd), lambda h, i: (1, 0, h)),
        ],
        out_specs=[
            pl.BlockSpec((rows, width), lambda h, i: (0, h * steps + i)),
            pl.BlockSpec((2, ext_rows, hd), lambda h, i: (0, 0, h)),
        ],
        out_shape=[
            jax.ShapeDtypeStruct((rows, qcols), jnp.bfloat16),
            jax.ShapeDtypeStruct((2, ext_rows, kcols), jnp.float32),
        ],
        compiler_params=pltpu.CompilerParams(dimension_semantics=("arbitrary", "arbitrary")),
        cost_estimate=pl.CostEstimate(
            flops=flops,
            transcendentals=rows * ext_rows * heads * group,
            bytes_accessed=3 * q.size * 2 + ext.size * 2 + ext.size * 4 + bias.size * 4,
        ),
    )(bias, q, g, ext, ext)


def scatter_layers(own_rows):
    sections = lax.axis_size("section")
    peers = lax.axis_size("tp")
    kinds, rows, cols = own_rows.shape
    pieces = own_rows.reshape(kinds, peers, sections, rows // (peers * sections), cols)
    pieces = jnp.swapaxes(pieces, 1, 2).reshape(kinds, sections * peers, rows // (peers * sections), cols)
    pieces = lax.all_to_all(pieces, ("section", "tp"), split_axis=1, concat_axis=1)
    pieces = pieces.reshape(kinds, sections, peers, rows // (peers * sections), cols)
    chunk = pieces[:, 0]
    for other in range(1, sections):
        chunk = chunk + pieces[:, other]
    return jnp.swapaxes(chunk, 1, 2)


def body(queries, upstream, shared_kv):
    local_kv = lax.all_to_all(shared_kv, "tp", split_axis=2, concat_axis=1, tiled=True)
    tok_rows = local_kv.shape[1]
    head_size = HD
    group_size = QH // KVH
    span_blocks = WINDOW // tok_rows
    score_scale = 1.0 / math.sqrt(head_size)
    earlier = [shifted(local_kv, "seq", span_blocks - offset) for offset in range(span_blocks)]
    extended = jnp.concatenate(earlier + [local_kv], axis=1)
    ext_rows = extended.shape[1]
    position = lax.axis_index("seq")
    row_ids = lax.broadcasted_iota(jnp.int32, (tok_rows, ext_rows), 0)
    key_ids = lax.broadcasted_iota(jnp.int32, (tok_rows, ext_rows), 1)
    allowed = (
        (key_ids >= row_ids + 1)
        & (key_ids <= row_ids + WINDOW)
        & (position * tok_rows - WINDOW + key_ids >= 0)
    )
    bias = jnp.where(allowed, 0.0, -jnp.inf).astype(jnp.float32)
    d_query_rows, grad_ext = attention_grads(
        bias,
        queries.reshape(tok_rows, -1),
        upstream.reshape(tok_rows, -1),
        extended,
        group_size,
        head_size,
        score_scale,
        2,
    )
    d_queries = d_query_rows.reshape(queries.shape)
    own_rows = grad_ext[:, span_blocks * tok_rows :, :]
    for offset in range(span_blocks):
        own_rows = own_rows + shifted(
            grad_ext[:, offset * tok_rows : (offset + 1) * tok_rows, :].astype(jnp.bfloat16),
            "seq",
            offset - span_blocks,
        ).astype(jnp.float32)
    chunk = scatter_layers(own_rows)
    kinds, rows, tp_peers, cols = chunk.shape
    d_shared_kv = lax.all_gather(chunk.reshape(kinds, rows, -1), "section", axis=1, tiled=True)
    return (d_queries, d_shared_kv)


def solution(mesh):
    in_specs = (P("section", "seq", "tp"), P("section", "seq", "tp"), P(None, ("seq", "tp"), None))
    out_specs = (P("section", "seq", "tp"), P(None, ("seq", "tp"), None))
    return jax.shard_map(body, mesh=mesh, in_specs=in_specs, out_specs=out_specs, check_vma=False)
```

```python
import functools
import math

import jax
import jax.numpy as jnp
from jax import lax
from jax.experimental import pallas as pl
from jax.experimental.pallas import tpu as pltpu
from jax.sharding import PartitionSpec as P

QH = 64
KVH = 8
HD = 128
WINDOW = 1024


def shifted(value, axis, by):
    peers = lax.axis_size(axis)
    pairs = [(i, i + by) for i in range(peers) if 0 <= i + by < peers]
    return lax.ppermute(value, axis, pairs)


def attn_kernel(bias_ref, q_ref, g_ref, k_ref, v_ref, dq_ref, dkv_ref, held, *, scale, hd, row_chunk, key_chunk):
    gi = pl.program_id(1)
    rows = q_ref.shape[0]
    ext_rows = k_ref.shape[0]
    key_parts = ext_rows // key_chunk
    nt = (((1,), (1,)), ((), ()))
    tn = (((0,), (0,)), ((), ()))

    @pl.when(gi == 0)
    def _():
        dkv_ref[...] = jnp.zeros_like(dkv_ref)

    for part in range(rows // row_chunk):
        lines = pl.ds(part * row_chunk, row_chunk)
        q = q_ref[lines, :]
        do = g_ref[lines, :]
        highest = jnp.full((row_chunk, 1), -jnp.inf, jnp.float32)
        for c in range(key_parts):
            keys = pl.ds(c * key_chunk, key_chunk)
            s = lax.dot_general(q, k_ref[keys, :], nt, preferred_element_type=jnp.float32) * scale
            s = s + bias_ref[lines, keys]
            held[c] = s
            highest = jnp.maximum(highest, jnp.max(s, axis=1, keepdims=True))
        total = jnp.zeros((row_chunk, 1), jnp.float32)
        for c in range(key_parts):
            w = jnp.exp(held[c] - highest)
            held[c] = w
            total = total + jnp.sum(w, axis=1, keepdims=True)
        inverse = 1.0 / total
        out = jnp.zeros((row_chunk, hd), jnp.float32)
        for c in range(key_parts):
            keys = pl.ds(c * key_chunk, key_chunk)
            p = held[c] * inverse
            held[c] = p
            out = out + jnp.dot(p.astype(jnp.bfloat16), v_ref[keys, :], preferred_element_type=jnp.float32)
        delta = jnp.sum(do.astype(jnp.float32) * out, axis=1, keepdims=True)
        dq = jnp.zeros((row_chunk, hd), jnp.float32)
        for c in range(key_parts):
            keys = pl.ds(c * key_chunk, key_chunk)
            v = v_ref[keys, :]
            k = k_ref[keys, :]
            p = held[c]
            dp = lax.dot_general(do, v, nt, preferred_element_type=jnp.float32)
            dsb = (p * (dp - delta)).astype(jnp.bfloat16)
            dq = dq + jnp.dot(dsb, k, preferred_element_type=jnp.float32)
            dkv_ref[0, keys, :] += lax.dot_general(dsb, q, tn, preferred_element_type=jnp.float32) * scale
            dkv_ref[1, keys, :] += lax.dot_general(p.astype(jnp.bfloat16), do, tn, preferred_element_type=jnp.float32)
        dq_ref[lines, :] = (dq * scale).astype(dq_ref.dtype)


def attention_grads(bias, q, g, ext, group, hd, scale, row_chunk, key_chunk):
    rows, qcols = q.shape
    _, ext_rows, kcols = ext.shape
    heads = kcols // hd
    flops = 6 * 2 * rows * ext_rows * hd * heads * group
    return pl.pallas_call(
        functools.partial(attn_kernel, scale=scale, hd=hd, row_chunk=row_chunk, key_chunk=key_chunk),
        grid=(heads, group),
        in_specs=[
            pl.BlockSpec((rows, ext_rows), lambda h, i: (0, 0)),
            pl.BlockSpec((rows, hd), lambda h, i: (0, h * group + i)),
            pl.BlockSpec((rows, hd), lambda h, i: (0, h * group + i)),
            pl.BlockSpec((None, ext_rows, hd), lambda h, i: (0, 0, h)),
            pl.BlockSpec((None, ext_rows, hd), lambda h, i: (1, 0, h)),
        ],
        out_specs=[
            pl.BlockSpec((rows, hd), lambda h, i: (0, h * group + i)),
            pl.BlockSpec((2, ext_rows, hd), lambda h, i: (0, 0, h)),
        ],
        out_shape=[
            jax.ShapeDtypeStruct((rows, qcols), jnp.bfloat16),
            jax.ShapeDtypeStruct((2, ext_rows, kcols), jnp.float32),
        ],
        scratch_shapes=[pltpu.VMEM((ext_rows // key_chunk, row_chunk, key_chunk), jnp.float32)],
        compiler_params=pltpu.CompilerParams(dimension_semantics=("arbitrary", "arbitrary")),
        cost_estimate=pl.CostEstimate(
            flops=flops,
            transcendentals=rows * ext_rows * heads * group,
            bytes_accessed=3 * q.size * 2 + ext.size * 2 + ext.size * 4 + bias.size * 4,
        ),
    )(bias, q, g, ext, ext)


def scatter_layers(own_rows):
    sections = lax.axis_size("section")
    peers = lax.axis_size("tp")
    kinds, rows, cols = own_rows.shape
    pieces = own_rows.reshape(kinds, peers, sections, rows // (peers * sections), cols)
    pieces = jnp.swapaxes(pieces, 1, 2).reshape(kinds, sections * peers, rows // (peers * sections), cols)
    pieces = lax.all_to_all(pieces, ("section", "tp"), split_axis=1, concat_axis=1)
    pieces = pieces.reshape(kinds, sections, peers, rows // (peers * sections), cols)
    chunk = pieces[:, 0]
    for other in range(1, sections):
        chunk = chunk + pieces[:, other]
    return jnp.swapaxes(chunk, 1, 2)


def body(queries, upstream, shared_kv):
    local_kv = lax.all_to_all(shared_kv, "tp", split_axis=2, concat_axis=1, tiled=True)
    tok_rows = local_kv.shape[1]
    head_size = HD
    group_size = QH // KVH
    span_blocks = WINDOW // tok_rows
    score_scale = 1.0 / math.sqrt(head_size)
    earlier = [shifted(local_kv, "seq", span_blocks - offset) for offset in range(span_blocks)]
    extended = jnp.concatenate(earlier + [local_kv], axis=1)
    ext_rows = extended.shape[1]
    position = lax.axis_index("seq")
    row_ids = lax.broadcasted_iota(jnp.int32, (tok_rows, ext_rows), 0)
    key_ids = lax.broadcasted_iota(jnp.int32, (tok_rows, ext_rows), 1)
    allowed = (
        (key_ids >= row_ids + 1)
        & (key_ids <= row_ids + WINDOW)
        & (position * tok_rows - WINDOW + key_ids >= 0)
    )
    bias = jnp.where(allowed, 0.0, -jnp.inf).astype(jnp.float32)
    d_query_rows, grad_ext = attention_grads(
        bias,
        queries.reshape(tok_rows, -1),
        upstream.reshape(tok_rows, -1),
        extended,
        group_size,
        head_size,
        score_scale,
        128,
        256,
    )
    d_queries = d_query_rows.reshape(queries.shape)
    own_rows = grad_ext[:, span_blocks * tok_rows :, :]
    for offset in range(span_blocks):
        own_rows = own_rows + shifted(
            grad_ext[:, offset * tok_rows : (offset + 1) * tok_rows, :].astype(jnp.bfloat16),
            "seq",
            offset - span_blocks,
        ).astype(jnp.float32)
    chunk = scatter_layers(own_rows)
    kinds, rows, tp_peers, cols = chunk.shape
    d_shared_kv = lax.all_gather(chunk.reshape(kinds, rows, -1), "section", axis=1, tiled=True)
    return (d_queries, d_shared_kv)


def solution(mesh):
    in_specs = (P("section", "seq", "tp"), P("section", "seq", "tp"), P(None, ("seq", "tp"), None))
    out_specs = (P("section", "seq", "tp"), P(None, ("seq", "tp"), None))
    return jax.shard_map(body, mesh=mesh, in_specs=in_specs, out_specs=out_specs, check_vma=False)
```

```python
import functools
import math

import jax
import jax.numpy as jnp
from jax import lax
from jax.experimental import pallas as pl
from jax.experimental.pallas import tpu as pltpu
from jax.sharding import PartitionSpec as P

QH = 64
KVH = 8
HD = 128
WINDOW = 1024


def shifted(value, axis, by):
    peers = lax.axis_size(axis)
    pairs = [(i, i + by) for i in range(peers) if 0 <= i + by < peers]
    return lax.ppermute(value, axis, pairs)


def attn_kernel(bias_ref, q_ref, g_ref, k_ref, v_ref, *rest, scale, hd, per_step):
    dq_ref, dkv_ref = rest[-2:]
    gi = pl.program_id(1)
    k = k_ref[...]
    v = v_ref[...]
    bias = bias_ref[...]
    nt = (((1,), (1,)), ((), ()))
    tn = (((0,), (0,)), ((), ()))
    dk = None
    dv = None
    for part in range(per_step):
        cols = slice(part * hd, (part + 1) * hd)
        q = q_ref[:, cols]
        do = g_ref[:, cols]
        s = lax.dot_general(q, k, nt, preferred_element_type=jnp.float32) * scale + bias
        m = jnp.max(s, axis=1, keepdims=True)
        w = jnp.exp(s - m)
        p = w * (1.0 / jnp.sum(w, axis=1, keepdims=True))
        pb = p.astype(jnp.bfloat16)
        o = jnp.dot(pb, v, preferred_element_type=jnp.float32)
        delta = jnp.sum(do.astype(jnp.float32) * o, axis=1, keepdims=True)
        dp = lax.dot_general(do, v, nt, preferred_element_type=jnp.float32)
        dsb = (p * (dp - delta)).astype(jnp.bfloat16)
        dq = jnp.dot(dsb, k, preferred_element_type=jnp.float32) * scale
        dq_ref[:, cols] = dq.astype(dq_ref.dtype)
        dk_part = lax.dot_general(dsb, q, tn, preferred_element_type=jnp.float32) * scale
        dv_part = lax.dot_general(pb, do, tn, preferred_element_type=jnp.float32)
        dk = dk_part if dk is None else dk + dk_part
        dv = dv_part if dv is None else dv + dv_part

    @pl.when(gi == 0)
    def _():
        dkv_ref[0] = dk
        dkv_ref[1] = dv

    @pl.when(gi > 0)
    def _():
        dkv_ref[0] += dk
        dkv_ref[1] += dv


def attention_grads(bias, q, g, ext, group, hd, scale, per_step, head0, heads, after=()):
    rows, _ = q.shape
    _, ext_rows, _ = ext.shape
    steps = group // per_step
    width = per_step * hd
    flops = 6 * 2 * rows * ext_rows * hd * heads * group
    return pl.pallas_call(
        functools.partial(attn_kernel, scale=scale, hd=hd, per_step=per_step),
        grid=(heads, steps),
        in_specs=[
            pl.BlockSpec((rows, ext_rows), lambda h, i: (0, 0)),
            pl.BlockSpec((rows, width), lambda h, i: (0, (head0 + h) * steps + i)),
            pl.BlockSpec((rows, width), lambda h, i: (0, (head0 + h) * steps + i)),
            pl.BlockSpec((None, ext_rows, hd), lambda h, i: (0, 0, head0 + h)),
            pl.BlockSpec((None, ext_rows, hd), lambda h, i: (1, 0, head0 + h)),
        ]
        + [pl.BlockSpec(memory_space=pl.ANY) for _ in after],
        out_specs=[
            pl.BlockSpec((rows, width), lambda h, i: (0, h * steps + i)),
            pl.BlockSpec((2, ext_rows, hd), lambda h, i: (0, 0, h)),
        ],
        out_shape=[
            jax.ShapeDtypeStruct((rows, heads * group * hd), jnp.bfloat16),
            jax.ShapeDtypeStruct((2, ext_rows, heads * hd), jnp.float32),
        ],
        compiler_params=pltpu.CompilerParams(dimension_semantics=("arbitrary", "arbitrary")),
        cost_estimate=pl.CostEstimate(
            flops=flops,
            transcendentals=rows * ext_rows * heads * group,
            bytes_accessed=(3 * rows * group * 2 + ext_rows * 2 * 6) * hd * heads + bias.size * 4,
        ),
    )(bias, q, g, ext, ext, *after)


def scatter_layers(own_rows):
    sections = lax.axis_size("section")
    peers = lax.axis_size("tp")
    kinds, rows, cols = own_rows.shape
    pieces = own_rows.reshape(kinds, peers, sections, rows // (peers * sections), cols)
    pieces = jnp.swapaxes(pieces, 1, 2).reshape(kinds, sections * peers, rows // (peers * sections), cols)
    pieces = lax.all_to_all(pieces, ("section", "tp"), split_axis=1, concat_axis=1)
    pieces = pieces.reshape(kinds, sections, peers, rows // (peers * sections), cols)
    chunk = pieces[:, 0]
    for other in range(1, sections):
        chunk = chunk + pieces[:, other]
    return jnp.swapaxes(chunk, 1, 2)


def body(queries, upstream, shared_kv):
    local_kv = lax.all_to_all(shared_kv, "tp", split_axis=2, concat_axis=1, tiled=True)
    tok_rows = local_kv.shape[1]
    head_size = HD
    group_size = QH // KVH
    span_blocks = WINDOW // tok_rows
    score_scale = 1.0 / math.sqrt(head_size)
    earlier = [shifted(local_kv, "seq", span_blocks - offset) for offset in range(span_blocks)]
    extended = jnp.concatenate(earlier + [local_kv], axis=1)
    ext_rows = extended.shape[1]
    position = lax.axis_index("seq")
    row_ids = lax.broadcasted_iota(jnp.int32, (tok_rows, ext_rows), 0)
    key_ids = lax.broadcasted_iota(jnp.int32, (tok_rows, ext_rows), 1)
    allowed = (
        (key_ids >= row_ids + 1)
        & (key_ids <= row_ids + WINDOW)
        & (position * tok_rows - WINDOW + key_ids >= 0)
    )
    bias = jnp.where(allowed, 0.0, -jnp.inf).astype(jnp.float32)
    query_rows = queries.reshape(tok_rows, -1)
    grad_rows = upstream.reshape(tok_rows, -1)
    local_heads = extended.shape[2] // head_size
    d_query_parts = []
    own_parts = []
    sent = []
    for kv_head in range(local_heads):
        d_query_part, grad_ext = attention_grads(
            bias, query_rows, grad_rows, extended, group_size, head_size, score_scale, 2, kv_head, 1, sent
        )
        d_query_parts.append(d_query_part)
        sent = [
            grad_ext[:, offset * tok_rows : (offset + 1) * tok_rows, :].astype(jnp.bfloat16)
            for offset in range(span_blocks)
        ]
        own_rows = grad_ext[:, span_blocks * tok_rows :, :]
        for offset in range(span_blocks):
            own_rows = own_rows + shifted(sent[offset], "seq", offset - span_blocks).astype(jnp.float32)
        own_parts.append(own_rows)
    d_queries = jnp.concatenate(d_query_parts, axis=1).reshape(queries.shape)
    own_rows = jnp.concatenate(own_parts, axis=2)
    chunk = scatter_layers(own_rows)
    kinds, rows, tp_peers, cols = chunk.shape
    d_shared_kv = lax.all_gather(chunk.reshape(kinds, rows, -1), "section", axis=1, tiled=True)
    return (d_queries, d_shared_kv)


def solution(mesh):
    in_specs = (P("section", "seq", "tp"), P("section", "seq", "tp"), P(None, ("seq", "tp"), None))
    out_specs = (P("section", "seq", "tp"), P(None, ("seq", "tp"), None))
    return jax.shard_map(body, mesh=mesh, in_specs=in_specs, out_specs=out_specs, check_vma=False)
```

```python
import functools
import math

import jax
import jax.numpy as jnp
from jax import lax
from jax.experimental import pallas as pl
from jax.experimental.pallas import tpu as pltpu
from jax.sharding import PartitionSpec as P

QH = 64
KVH = 8
HD = 128
WINDOW = 1024


def shifted(value, axis, by):
    peers = lax.axis_size(axis)
    pairs = [(i, i + by) for i in range(peers) if 0 <= i + by < peers]
    return lax.ppermute(value, axis, pairs)


def attn_kernel(bias_ref, q_ref, g_ref, k_ref, v_ref, *rest, scale, hd, per_step):
    dq_ref, dkv_ref = rest[-2:]
    gi = pl.program_id(1)
    k = k_ref[...]
    v = v_ref[...]
    bias = bias_ref[...]
    nt = (((1,), (1,)), ((), ()))
    tn = (((0,), (0,)), ((), ()))
    dk = None
    dv = None
    for part in range(per_step):
        cols = slice(part * hd, (part + 1) * hd)
        q = q_ref[:, cols]
        do = g_ref[:, cols]
        s = lax.dot_general(q, k, nt, preferred_element_type=jnp.float32) * scale + bias
        m = jnp.max(s, axis=1, keepdims=True)
        w = jnp.exp(s - m)
        p = w * (1.0 / jnp.sum(w, axis=1, keepdims=True))
        pb = p.astype(jnp.bfloat16)
        o = jnp.dot(pb, v, preferred_element_type=jnp.float32)
        delta = jnp.sum(do.astype(jnp.float32) * o, axis=1, keepdims=True)
        dp = lax.dot_general(do, v, nt, preferred_element_type=jnp.float32)
        dsb = (p * (dp - delta)).astype(jnp.bfloat16)
        dq = jnp.dot(dsb, k, preferred_element_type=jnp.float32) * scale
        dq_ref[:, cols] = dq.astype(dq_ref.dtype)
        dk_part = lax.dot_general(dsb, q, tn, preferred_element_type=jnp.float32) * scale
        dv_part = lax.dot_general(pb, do, tn, preferred_element_type=jnp.float32)
        dk = dk_part if dk is None else dk + dk_part
        dv = dv_part if dv is None else dv + dv_part

    @pl.when(gi == 0)
    def _():
        dkv_ref[0] = dk
        dkv_ref[1] = dv

    @pl.when(gi > 0)
    def _():
        dkv_ref[0] += dk
        dkv_ref[1] += dv


def attention_grads(bias, q, g, ext, group, hd, scale, per_step, head0, heads, after=()):
    rows, _ = q.shape
    _, ext_rows, _ = ext.shape
    steps = group // per_step
    width = per_step * hd
    flops = 6 * 2 * rows * ext_rows * hd * heads * group
    return pl.pallas_call(
        functools.partial(attn_kernel, scale=scale, hd=hd, per_step=per_step),
        grid=(heads, steps),
        in_specs=[
            pl.BlockSpec((rows, ext_rows), lambda h, i: (0, 0)),
            pl.BlockSpec((rows, width), lambda h, i: (0, (head0 + h) * steps + i)),
            pl.BlockSpec((rows, width), lambda h, i: (0, (head0 + h) * steps + i)),
            pl.BlockSpec((None, ext_rows, hd), lambda h, i: (0, 0, head0 + h)),
            pl.BlockSpec((None, ext_rows, hd), lambda h, i: (1, 0, head0 + h)),
        ]
        + [pl.BlockSpec(memory_space=pl.ANY) for _ in after],
        out_specs=[
            pl.BlockSpec((rows, width), lambda h, i: (0, h * steps + i)),
            pl.BlockSpec((2, ext_rows, hd), lambda h, i: (0, 0, h)),
        ],
        out_shape=[
            jax.ShapeDtypeStruct((rows, heads * group * hd), jnp.bfloat16),
            jax.ShapeDtypeStruct((2, ext_rows, heads * hd), jnp.float32),
        ],
        compiler_params=pltpu.CompilerParams(dimension_semantics=("arbitrary", "arbitrary")),
        cost_estimate=pl.CostEstimate(
            flops=flops,
            transcendentals=rows * ext_rows * heads * group,
            bytes_accessed=(3 * rows * group * 2 + ext_rows * 2 * 6) * hd * heads + bias.size * 4,
        ),
    )(bias, q, g, ext, ext, *after)


def scatter_layers(own_rows):
    sections = lax.axis_size("section")
    peers = lax.axis_size("tp")
    kinds, rows, cols = own_rows.shape
    pieces = own_rows.reshape(kinds, peers, sections, rows // (peers * sections), cols)
    pieces = jnp.swapaxes(pieces, 1, 2).reshape(kinds, sections * peers, rows // (peers * sections), cols)
    pieces = lax.all_to_all(pieces, ("section", "tp"), split_axis=1, concat_axis=1)
    pieces = pieces.reshape(kinds, sections, peers, rows // (peers * sections), cols)
    chunk = pieces[:, 0]
    for other in range(1, sections):
        chunk = chunk + pieces[:, other]
    return jnp.swapaxes(chunk, 1, 2)


def body(queries, upstream, shared_kv):
    local_kv = lax.all_to_all(shared_kv, "tp", split_axis=2, concat_axis=1, tiled=True)
    tok_rows = local_kv.shape[1]
    head_size = HD
    group_size = QH // KVH
    span_blocks = WINDOW // tok_rows
    score_scale = 1.0 / math.sqrt(head_size)
    sections = lax.axis_size("section")
    quarter = tok_rows // sections
    mine = lax.dynamic_slice_in_dim(local_kv, lax.axis_index("section") * quarter, quarter, axis=1)
    earlier = jnp.stack([shifted(mine, "seq", span_blocks - offset) for offset in range(span_blocks)], axis=1)
    gathered = lax.all_gather(earlier, "section", axis=2)
    kinds, _, _, _, cols = gathered.shape
    extended = jnp.concatenate([gathered.reshape(kinds, span_blocks * tok_rows, cols), local_kv], axis=1)
    ext_rows = extended.shape[1]
    position = lax.axis_index("seq")
    row_ids = lax.broadcasted_iota(jnp.int32, (tok_rows, ext_rows), 0)
    key_ids = lax.broadcasted_iota(jnp.int32, (tok_rows, ext_rows), 1)
    allowed = (
        (key_ids >= row_ids + 1)
        & (key_ids <= row_ids + WINDOW)
        & (position * tok_rows - WINDOW + key_ids >= 0)
    )
    bias = jnp.where(allowed, 0.0, -jnp.inf).astype(jnp.float32)
    query_rows = queries.reshape(tok_rows, -1)
    grad_rows = upstream.reshape(tok_rows, -1)
    local_heads = extended.shape[2] // head_size
    d_query_parts = []
    own_parts = []
    sent = []
    for kv_head in range(local_heads):
        d_query_part, grad_ext = attention_grads(
            bias, query_rows, grad_rows, extended, group_size, head_size, score_scale, 2, kv_head, 1, sent
        )
        d_query_parts.append(d_query_part)
        sent = [
            grad_ext[:, offset * tok_rows : (offset + 1) * tok_rows, :].astype(jnp.bfloat16)
            for offset in range(span_blocks)
        ]
        own_rows = grad_ext[:, span_blocks * tok_rows :, :]
        for offset in range(span_blocks):
            own_rows = own_rows + shifted(sent[offset], "seq", offset - span_blocks).astype(jnp.float32)
        own_parts.append(own_rows)
    d_queries = jnp.concatenate(d_query_parts, axis=1).reshape(queries.shape)
    own_rows = jnp.concatenate(own_parts, axis=2)
    chunk = scatter_layers(own_rows)
    kinds, rows, tp_peers, cols = chunk.shape
    d_shared_kv = lax.all_gather(chunk.reshape(kinds, rows, -1), "section", axis=1, tiled=True)
    return (d_queries, d_shared_kv)


def solution(mesh):
    in_specs = (P("section", "seq", "tp"), P("section", "seq", "tp"), P(None, ("seq", "tp"), None))
    out_specs = (P("section", "seq", "tp"), P(None, ("seq", "tp"), None))
    return jax.shard_map(body, mesh=mesh, in_specs=in_specs, out_specs=out_specs, check_vma=False)
```

```python
import functools
import math

import jax
import jax.numpy as jnp
from jax import lax
from jax.experimental import pallas as pl
from jax.experimental.pallas import tpu as pltpu
from jax.sharding import PartitionSpec as P

QH = 64
KVH = 8
HD = 128
WINDOW = 1024


def shifted(value, axis, by):
    peers = lax.axis_size(axis)
    pairs = [(i, i + by) for i in range(peers) if 0 <= i + by < peers]
    return lax.ppermute(value, axis, pairs)


def attn_kernel(bias_ref, q_ref, g_ref, k_ref, v_ref, *rest, scale, hd, per_step):
    dq_ref, dkv_ref = rest[-2:]
    gi = pl.program_id(1)
    k = k_ref[...]
    v = v_ref[...]
    bias = bias_ref[...]
    nt = (((1,), (1,)), ((), ()))
    tn = (((0,), (0,)), ((), ()))
    dk = None
    dv = None
    for part in range(per_step):
        cols = slice(part * hd, (part + 1) * hd)
        q = q_ref[:, cols]
        do = g_ref[:, cols]
        s = lax.dot_general(q, k, nt, preferred_element_type=jnp.float32) * scale + bias
        m = jnp.max(s, axis=1, keepdims=True)
        w = jnp.exp(s - m)
        p = w * (1.0 / jnp.sum(w, axis=1, keepdims=True))
        pb = p.astype(jnp.bfloat16)
        o = jnp.dot(pb, v, preferred_element_type=jnp.float32)
        delta = jnp.sum(do.astype(jnp.float32) * o, axis=1, keepdims=True)
        dp = lax.dot_general(do, v, nt, preferred_element_type=jnp.float32)
        dsb = (p * (dp - delta)).astype(jnp.bfloat16)
        dq = jnp.dot(dsb, k, preferred_element_type=jnp.float32) * scale
        dq_ref[:, cols] = dq.astype(dq_ref.dtype)
        dk_part = lax.dot_general(dsb, q, tn, preferred_element_type=jnp.float32) * scale
        dv_part = lax.dot_general(pb, do, tn, preferred_element_type=jnp.float32)
        dk = dk_part if dk is None else dk + dk_part
        dv = dv_part if dv is None else dv + dv_part

    @pl.when(gi == 0)
    def _():
        dkv_ref[0] = dk
        dkv_ref[1] = dv

    @pl.when(gi > 0)
    def _():
        dkv_ref[0] += dk
        dkv_ref[1] += dv


def attention_grads(bias, q, g, ext, group, hd, scale, per_step, head0, heads, after=()):
    rows, _ = q.shape
    _, ext_rows, _ = ext.shape
    steps = group // per_step
    width = per_step * hd
    flops = 6 * 2 * rows * ext_rows * hd * heads * group
    return pl.pallas_call(
        functools.partial(attn_kernel, scale=scale, hd=hd, per_step=per_step),
        grid=(heads, steps),
        in_specs=[
            pl.BlockSpec((rows, ext_rows), lambda h, i: (0, 0)),
            pl.BlockSpec((rows, width), lambda h, i: (0, (head0 + h) * steps + i)),
            pl.BlockSpec((rows, width), lambda h, i: (0, (head0 + h) * steps + i)),
            pl.BlockSpec((None, ext_rows, hd), lambda h, i: (0, 0, head0 + h)),
            pl.BlockSpec((None, ext_rows, hd), lambda h, i: (1, 0, head0 + h)),
        ]
        + [pl.BlockSpec(memory_space=pl.ANY) for _ in after],
        out_specs=[
            pl.BlockSpec((rows, width), lambda h, i: (0, h * steps + i)),
            pl.BlockSpec((2, ext_rows, hd), lambda h, i: (0, 0, h)),
        ],
        out_shape=[
            jax.ShapeDtypeStruct((rows, heads * group * hd), jnp.bfloat16),
            jax.ShapeDtypeStruct((2, ext_rows, heads * hd), jnp.float32),
        ],
        compiler_params=pltpu.CompilerParams(dimension_semantics=("arbitrary", "arbitrary")),
        cost_estimate=pl.CostEstimate(
            flops=flops,
            transcendentals=rows * ext_rows * heads * group,
            bytes_accessed=(3 * rows * group * 2 + ext_rows * 2 * 6) * hd * heads + bias.size * 4,
        ),
    )(bias, q, g, ext, ext, *after)


def scatter_layers(own_rows):
    sections = lax.axis_size("section")
    peers = lax.axis_size("tp")
    kinds, rows, cols = own_rows.shape
    pieces = own_rows.reshape(kinds, peers, sections, rows // (peers * sections), cols)
    pieces = jnp.swapaxes(pieces, 1, 2).reshape(kinds, sections * peers, rows // (peers * sections), cols)
    pieces = lax.all_to_all(pieces.astype(jnp.bfloat16), ("section", "tp"), split_axis=1, concat_axis=1)
    pieces = pieces.astype(jnp.float32).reshape(kinds, sections, peers, rows // (peers * sections), cols)
    chunk = pieces[:, 0]
    for other in range(1, sections):
        chunk = chunk + pieces[:, other]
    return jnp.swapaxes(chunk, 1, 2)


def body(queries, upstream, shared_kv):
    local_kv = lax.all_to_all(shared_kv, "tp", split_axis=2, concat_axis=1, tiled=True)
    tok_rows = local_kv.shape[1]
    head_size = HD
    group_size = QH // KVH
    span_blocks = WINDOW // tok_rows
    score_scale = 1.0 / math.sqrt(head_size)
    earlier = [shifted(local_kv, "seq", span_blocks - offset) for offset in range(span_blocks)]
    extended = jnp.concatenate(earlier + [local_kv], axis=1)
    ext_rows = extended.shape[1]
    position = lax.axis_index("seq")
    row_ids = lax.broadcasted_iota(jnp.int32, (tok_rows, ext_rows), 0)
    key_ids = lax.broadcasted_iota(jnp.int32, (tok_rows, ext_rows), 1)
    allowed = (
        (key_ids >= row_ids + 1)
        & (key_ids <= row_ids + WINDOW)
        & (position * tok_rows - WINDOW + key_ids >= 0)
    )
    bias = jnp.where(allowed, 0.0, -jnp.inf).astype(jnp.float32)
    query_rows = queries.reshape(tok_rows, -1)
    grad_rows = upstream.reshape(tok_rows, -1)
    local_heads = extended.shape[2] // head_size
    d_query_parts = []
    own_parts = []
    sent = []
    for kv_head in range(local_heads):
        d_query_part, grad_ext = attention_grads(
            bias, query_rows, grad_rows, extended, group_size, head_size, score_scale, 2, kv_head, 1, sent
        )
        d_query_parts.append(d_query_part)
        sent = [
            grad_ext[:, offset * tok_rows : (offset + 1) * tok_rows, :].astype(jnp.bfloat16)
            for offset in range(span_blocks)
        ]
        own_rows = grad_ext[:, span_blocks * tok_rows :, :]
        for offset in range(span_blocks):
            own_rows = own_rows + shifted(sent[offset], "seq", offset - span_blocks).astype(jnp.float32)
        own_parts.append(own_rows)
    d_queries = jnp.concatenate(d_query_parts, axis=1).reshape(queries.shape)
    own_rows = jnp.concatenate(own_parts, axis=2)
    chunk = scatter_layers(own_rows)
    kinds, rows, tp_peers, cols = chunk.shape
    d_shared_kv = lax.all_gather(
        chunk.reshape(kinds, rows, -1).astype(jnp.bfloat16), "section", axis=1, tiled=True
    ).astype(jnp.float32)
    return (d_queries, d_shared_kv)


def solution(mesh):
    in_specs = (P("section", "seq", "tp"), P("section", "seq", "tp"), P(None, ("seq", "tp"), None))
    out_specs = (P("section", "seq", "tp"), P(None, ("seq", "tp"), None))
    return jax.shard_map(body, mesh=mesh, in_specs=in_specs, out_specs=out_specs, check_vma=False)
```

```python
import functools
import math

import jax
import jax.numpy as jnp
from jax import lax
from jax.experimental import pallas as pl
from jax.experimental.pallas import tpu as pltpu
from jax.sharding import PartitionSpec as P

QH = 64
KVH = 8
HD = 128
WINDOW = 1024


def shifted(value, axis, by):
    peers = lax.axis_size(axis)
    pairs = [(i, i + by) for i in range(peers) if 0 <= i + by < peers]
    return lax.ppermute(value, axis, pairs)


def attn_kernel(bias_ref, q_ref, g_ref, k_ref, v_ref, *rest, scale, hd, per_step):
    dq_ref, dkv_ref = rest[-2:]
    gi = pl.program_id(1)
    k = k_ref[...]
    v = v_ref[...]
    bias = bias_ref[...]
    nt = (((1,), (1,)), ((), ()))
    tn = (((0,), (0,)), ((), ()))
    dk = None
    dv = None
    for part in range(per_step):
        cols = slice(part * hd, (part + 1) * hd)
        q = q_ref[:, cols]
        do = g_ref[:, cols]
        s = lax.dot_general(q, k, nt, preferred_element_type=jnp.float32) * scale + bias
        m = jnp.max(s, axis=1, keepdims=True)
        w = jnp.exp(s - m)
        p = w * (1.0 / jnp.sum(w, axis=1, keepdims=True))
        pb = p.astype(jnp.bfloat16)
        o = jnp.dot(pb, v, preferred_element_type=jnp.float32)
        delta = jnp.sum(do.astype(jnp.float32) * o, axis=1, keepdims=True)
        dp = lax.dot_general(do, v, nt, preferred_element_type=jnp.float32)
        dsb = (p * (dp - delta)).astype(jnp.bfloat16)
        dq = jnp.dot(dsb, k, preferred_element_type=jnp.float32) * scale
        dq_ref[:, cols] = dq.astype(dq_ref.dtype)
        dk_part = lax.dot_general(q, dsb, tn, preferred_element_type=jnp.float32) * scale
        dv_part = lax.dot_general(do, pb, tn, preferred_element_type=jnp.float32)
        dk = dk_part if dk is None else dk + dk_part
        dv = dv_part if dv is None else dv + dv_part

    @pl.when(gi == 0)
    def _():
        dkv_ref[0] = dk
        dkv_ref[1] = dv

    @pl.when(gi > 0)
    def _():
        dkv_ref[0] += dk
        dkv_ref[1] += dv


def attention_grads(bias, q, g, ext, group, hd, scale, per_step, head0, heads, after=()):
    rows, _ = q.shape
    _, ext_rows, _ = ext.shape
    steps = group // per_step
    width = per_step * hd
    flops = 6 * 2 * rows * ext_rows * hd * heads * group
    return pl.pallas_call(
        functools.partial(attn_kernel, scale=scale, hd=hd, per_step=per_step),
        grid=(heads, steps),
        in_specs=[
            pl.BlockSpec((rows, ext_rows), lambda h, i: (0, 0)),
            pl.BlockSpec((rows, width), lambda h, i: (0, (head0 + h) * steps + i)),
            pl.BlockSpec((rows, width), lambda h, i: (0, (head0 + h) * steps + i)),
            pl.BlockSpec((None, ext_rows, hd), lambda h, i: (0, 0, head0 + h)),
            pl.BlockSpec((None, ext_rows, hd), lambda h, i: (1, 0, head0 + h)),
        ]
        + [pl.BlockSpec(memory_space=pl.ANY) for _ in after],
        out_specs=[
            pl.BlockSpec((rows, width), lambda h, i: (0, h * steps + i)),
            pl.BlockSpec((2, hd, ext_rows), lambda h, i: (0, h, 0)),
        ],
        out_shape=[
            jax.ShapeDtypeStruct((rows, heads * group * hd), jnp.bfloat16),
            jax.ShapeDtypeStruct((2, heads * hd, ext_rows), jnp.float32),
        ],
        compiler_params=pltpu.CompilerParams(dimension_semantics=("arbitrary", "arbitrary")),
        cost_estimate=pl.CostEstimate(
            flops=flops,
            transcendentals=rows * ext_rows * heads * group,
            bytes_accessed=(3 * rows * group * 2 + ext_rows * 2 * 6) * hd * heads + bias.size * 4,
        ),
    )(bias, q, g, ext, ext, *after)


def scatter_layers(own_rows):
    sections = lax.axis_size("section")
    peers = lax.axis_size("tp")
    kinds, rows, cols = own_rows.shape
    pieces = own_rows.reshape(kinds, peers, sections, rows // (peers * sections), cols)
    pieces = jnp.swapaxes(pieces, 1, 2).reshape(kinds, sections * peers, rows // (peers * sections), cols)
    pieces = lax.all_to_all(pieces.astype(jnp.bfloat16), ("section", "tp"), split_axis=1, concat_axis=1)
    pieces = pieces.astype(jnp.float32).reshape(kinds, sections, peers, rows // (peers * sections), cols)
    chunk = pieces[:, 0]
    for other in range(1, sections):
        chunk = chunk + pieces[:, other]
    return jnp.swapaxes(chunk, 1, 2)


def body(queries, upstream, shared_kv):
    local_kv = lax.all_to_all(shared_kv, "tp", split_axis=2, concat_axis=1, tiled=True)
    tok_rows = local_kv.shape[1]
    head_size = HD
    group_size = QH // KVH
    span_blocks = WINDOW // tok_rows
    score_scale = 1.0 / math.sqrt(head_size)
    earlier = [shifted(local_kv, "seq", span_blocks - offset) for offset in range(span_blocks)]
    extended = jnp.concatenate(earlier + [local_kv], axis=1)
    ext_rows = extended.shape[1]
    position = lax.axis_index("seq")
    row_ids = lax.broadcasted_iota(jnp.int32, (tok_rows, ext_rows), 0)
    key_ids = lax.broadcasted_iota(jnp.int32, (tok_rows, ext_rows), 1)
    allowed = (
        (key_ids >= row_ids + 1)
        & (key_ids <= row_ids + WINDOW)
        & (position * tok_rows - WINDOW + key_ids >= 0)
    )
    bias = jnp.where(allowed, 0.0, -jnp.inf).astype(jnp.float32)
    query_rows = queries.reshape(tok_rows, -1)
    grad_rows = upstream.reshape(tok_rows, -1)
    local_heads = extended.shape[2] // head_size
    d_query_parts = []
    own_parts = []
    sent = []
    for kv_head in range(local_heads):
        d_query_part, grad_ext = attention_grads(
            bias, query_rows, grad_rows, extended, group_size, head_size, score_scale, 2, kv_head, 1, sent
        )
        grad_ext = jnp.swapaxes(grad_ext, 1, 2)
        d_query_parts.append(d_query_part)
        sent = [
            grad_ext[:, offset * tok_rows : (offset + 1) * tok_rows, :].astype(jnp.bfloat16)
            for offset in range(span_blocks)
        ]
        own_rows = grad_ext[:, span_blocks * tok_rows :, :]
        for offset in range(span_blocks):
            own_rows = own_rows + shifted(sent[offset], "seq", offset - span_blocks).astype(jnp.float32)
        own_parts.append(own_rows)
    d_queries = jnp.concatenate(d_query_parts, axis=1).reshape(queries.shape)
    own_rows = jnp.concatenate(own_parts, axis=2)
    chunk = scatter_layers(own_rows)
    kinds, rows, tp_peers, cols = chunk.shape
    d_shared_kv = lax.all_gather(
        chunk.reshape(kinds, rows, -1).astype(jnp.bfloat16), "section", axis=1, tiled=True
    ).astype(jnp.float32)
    return (d_queries, d_shared_kv)


def solution(mesh):
    in_specs = (P("section", "seq", "tp"), P("section", "seq", "tp"), P(None, ("seq", "tp"), None))
    out_specs = (P("section", "seq", "tp"), P(None, ("seq", "tp"), None))
    return jax.shard_map(body, mesh=mesh, in_specs=in_specs, out_specs=out_specs, check_vma=False)
```

```python
import functools
import math

import jax
import jax.numpy as jnp
from jax import lax
from jax.experimental import pallas as pl
from jax.experimental.pallas import tpu as pltpu
from jax.sharding import PartitionSpec as P

QH = 64
KVH = 8
HD = 128
WINDOW = 1024


def shifted(value, axis, by):
    peers = lax.axis_size(axis)
    pairs = [(i, i + by) for i in range(peers) if 0 <= i + by < peers]
    return lax.ppermute(value, axis, pairs)


def attn_kernel(bias_ref, q_ref, g_ref, kt_ref, vt_ref, *rest, scale, hd, per_step):
    dq_ref, dkv_ref = rest[-2:]
    gi = pl.program_id(1)
    kt = kt_ref[...]
    vt = vt_ref[...]
    bias = bias_ref[...]
    nt = (((1,), (1,)), ((), ()))
    tn = (((0,), (0,)), ((), ()))
    dk = None
    dv = None
    for part in range(per_step):
        cols = slice(part * hd, (part + 1) * hd)
        q = q_ref[:, cols]
        do = g_ref[:, cols]
        s = jnp.dot(q, kt, preferred_element_type=jnp.float32) * scale + bias
        m = jnp.max(s, axis=1, keepdims=True)
        w = jnp.exp(s - m)
        p = w * (1.0 / jnp.sum(w, axis=1, keepdims=True))
        pb = p.astype(jnp.bfloat16)
        o = lax.dot_general(vt, pb, nt, preferred_element_type=jnp.float32).T
        delta = jnp.sum(do.astype(jnp.float32) * o, axis=1, keepdims=True)
        dp = jnp.dot(do, vt, preferred_element_type=jnp.float32)
        dsb = (p * (dp - delta)).astype(jnp.bfloat16)
        dq = lax.dot_general(kt, dsb, nt, preferred_element_type=jnp.float32).T * scale
        dq_ref[:, cols] = dq.astype(dq_ref.dtype)
        dk_part = lax.dot_general(q, dsb, tn, preferred_element_type=jnp.float32) * scale
        dv_part = lax.dot_general(do, pb, tn, preferred_element_type=jnp.float32)
        dk = dk_part if dk is None else dk + dk_part
        dv = dv_part if dv is None else dv + dv_part

    @pl.when(gi == 0)
    def _():
        dkv_ref[0] = dk
        dkv_ref[1] = dv

    @pl.when(gi > 0)
    def _():
        dkv_ref[0] += dk
        dkv_ref[1] += dv


def attention_grads(bias, q, g, ext, group, hd, scale, per_step, head0, heads, after=()):
    rows, _ = q.shape
    _, _, ext_rows = ext.shape
    steps = group // per_step
    width = per_step * hd
    flops = 6 * 2 * rows * ext_rows * hd * heads * group
    return pl.pallas_call(
        functools.partial(attn_kernel, scale=scale, hd=hd, per_step=per_step),
        grid=(heads, steps),
        in_specs=[
            pl.BlockSpec((rows, ext_rows), lambda h, i: (0, 0)),
            pl.BlockSpec((rows, width), lambda h, i: (0, (head0 + h) * steps + i)),
            pl.BlockSpec((rows, width), lambda h, i: (0, (head0 + h) * steps + i)),
            pl.BlockSpec((None, hd, ext_rows), lambda h, i: (0, head0 + h, 0)),
            pl.BlockSpec((None, hd, ext_rows), lambda h, i: (1, head0 + h, 0)),
        ]
        + [pl.BlockSpec(memory_space=pl.ANY) for _ in after],
        out_specs=[
            pl.BlockSpec((rows, width), lambda h, i: (0, h * steps + i)),
            pl.BlockSpec((2, hd, ext_rows), lambda h, i: (0, h, 0)),
        ],
        out_shape=[
            jax.ShapeDtypeStruct((rows, heads * group * hd), jnp.bfloat16),
            jax.ShapeDtypeStruct((2, heads * hd, ext_rows), jnp.float32),
        ],
        compiler_params=pltpu.CompilerParams(dimension_semantics=("arbitrary", "arbitrary")),
        cost_estimate=pl.CostEstimate(
            flops=flops,
            transcendentals=rows * ext_rows * heads * group,
            bytes_accessed=(3 * rows * group * 2 + ext_rows * 2 * 6) * hd * heads + bias.size * 4,
        ),
    )(bias, q, g, ext, ext, *after)


def scatter_layers(own_rows):
    sections = lax.axis_size("section")
    peers = lax.axis_size("tp")
    kinds, rows, cols = own_rows.shape
    pieces = own_rows.reshape(kinds, peers, sections, rows // (peers * sections), cols)
    pieces = jnp.swapaxes(pieces, 1, 2).reshape(kinds, sections * peers, rows // (peers * sections), cols)
    pieces = lax.all_to_all(pieces.astype(jnp.bfloat16), ("section", "tp"), split_axis=1, concat_axis=1)
    pieces = pieces.astype(jnp.float32).reshape(kinds, sections, peers, rows // (peers * sections), cols)
    chunk = pieces[:, 0]
    for other in range(1, sections):
        chunk = chunk + pieces[:, other]
    return jnp.swapaxes(chunk, 1, 2)


def body(queries, upstream, shared_kv):
    local_kv = lax.all_to_all(shared_kv, "tp", split_axis=2, concat_axis=1, tiled=True)
    tok_rows = local_kv.shape[1]
    head_size = HD
    group_size = QH // KVH
    span_blocks = WINDOW // tok_rows
    score_scale = 1.0 / math.sqrt(head_size)
    earlier = [shifted(local_kv, "seq", span_blocks - offset) for offset in range(span_blocks)]
    extended = jnp.concatenate(earlier + [local_kv], axis=1)
    ext_rows = extended.shape[1]
    position = lax.axis_index("seq")
    row_ids = lax.broadcasted_iota(jnp.int32, (tok_rows, ext_rows), 0)
    key_ids = lax.broadcasted_iota(jnp.int32, (tok_rows, ext_rows), 1)
    allowed = (
        (key_ids >= row_ids + 1)
        & (key_ids <= row_ids + WINDOW)
        & (position * tok_rows - WINDOW + key_ids >= 0)
    )
    bias = jnp.where(allowed, 0.0, -jnp.inf).astype(jnp.float32)
    extended = jnp.swapaxes(extended, 1, 2)
    query_rows = queries.reshape(tok_rows, -1)
    grad_rows = upstream.reshape(tok_rows, -1)
    local_heads = extended.shape[1] // head_size
    d_query_parts = []
    own_parts = []
    sent = []
    for kv_head in range(local_heads):
        d_query_part, grad_ext = attention_grads(
            bias, query_rows, grad_rows, extended, group_size, head_size, score_scale, 2, kv_head, 1, sent
        )
        grad_ext = jnp.swapaxes(grad_ext, 1, 2)
        d_query_parts.append(d_query_part)
        sent = [
            grad_ext[:, offset * tok_rows : (offset + 1) * tok_rows, :].astype(jnp.bfloat16)
            for offset in range(span_blocks)
        ]
        own_rows = grad_ext[:, span_blocks * tok_rows :, :]
        for offset in range(span_blocks):
            own_rows = own_rows + shifted(sent[offset], "seq", offset - span_blocks).astype(jnp.float32)
        own_parts.append(own_rows)
    d_queries = jnp.concatenate(d_query_parts, axis=1).reshape(queries.shape)
    own_rows = jnp.concatenate(own_parts, axis=2)
    chunk = scatter_layers(own_rows)
    kinds, rows, tp_peers, cols = chunk.shape
    d_shared_kv = lax.all_gather(
        chunk.reshape(kinds, rows, -1).astype(jnp.bfloat16), "section", axis=1, tiled=True
    ).astype(jnp.float32)
    return (d_queries, d_shared_kv)


def solution(mesh):
    in_specs = (P("section", "seq", "tp"), P("section", "seq", "tp"), P(None, ("seq", "tp"), None))
    out_specs = (P("section", "seq", "tp"), P(None, ("seq", "tp"), None))
    return jax.shard_map(body, mesh=mesh, in_specs=in_specs, out_specs=out_specs, check_vma=False)
```

```python
import functools
import math

import jax
import jax.numpy as jnp
from jax import lax
from jax.experimental import pallas as pl
from jax.experimental.pallas import tpu as pltpu
from jax.sharding import PartitionSpec as P

QH = 64
KVH = 8
HD = 128
WINDOW = 1024


def shifted(value, axis, by):
    peers = lax.axis_size(axis)
    pairs = [(i, i + by) for i in range(peers) if 0 <= i + by < peers]
    return lax.ppermute(value, axis, pairs)


def attn_kernel(bias_ref, q_ref, g_ref, k_ref, v_ref, kt_ref, vt_ref, *rest, scale, hd, per_step):
    dq_ref, dkv_ref = rest[-2:]
    gi = pl.program_id(1)
    k = k_ref[...]
    v = v_ref[...]
    kt = kt_ref[...]
    vt = vt_ref[...]
    bias = bias_ref[...]
    nt = (((1,), (1,)), ((), ()))
    tn = (((0,), (0,)), ((), ()))
    dk = None
    dv = None
    for part in range(per_step):
        cols = slice(part * hd, (part + 1) * hd)
        q = q_ref[:, cols]
        do = g_ref[:, cols]
        s = jnp.dot(q, kt, preferred_element_type=jnp.float32) * scale + bias
        m = jnp.max(s, axis=1, keepdims=True)
        w = jnp.exp(s - m)
        p = w * (1.0 / jnp.sum(w, axis=1, keepdims=True))
        pb = p.astype(jnp.bfloat16)
        o = jnp.dot(pb, v, preferred_element_type=jnp.float32)
        delta = jnp.sum(do.astype(jnp.float32) * o, axis=1, keepdims=True)
        dp = jnp.dot(do, vt, preferred_element_type=jnp.float32)
        dsb = (p * (dp - delta)).astype(jnp.bfloat16)
        dq = jnp.dot(dsb, k, preferred_element_type=jnp.float32) * scale
        dq_ref[:, cols] = dq.astype(dq_ref.dtype)
        dk_part = lax.dot_general(q, dsb, tn, preferred_element_type=jnp.float32) * scale
        dv_part = lax.dot_general(do, pb, tn, preferred_element_type=jnp.float32)
        dk = dk_part if dk is None else dk + dk_part
        dv = dv_part if dv is None else dv + dv_part

    @pl.when(gi == 0)
    def _():
        dkv_ref[0] = dk
        dkv_ref[1] = dv

    @pl.when(gi > 0)
    def _():
        dkv_ref[0] += dk
        dkv_ref[1] += dv


def attention_grads(bias, q, g, ext, ext_t, group, hd, scale, per_step, head0, heads, after=()):
    rows, _ = q.shape
    _, ext_rows, _ = ext.shape
    steps = group // per_step
    width = per_step * hd
    flops = 6 * 2 * rows * ext_rows * hd * heads * group
    return pl.pallas_call(
        functools.partial(attn_kernel, scale=scale, hd=hd, per_step=per_step),
        grid=(heads, steps),
        in_specs=[
            pl.BlockSpec((rows, ext_rows), lambda h, i: (0, 0)),
            pl.BlockSpec((rows, width), lambda h, i: (0, (head0 + h) * steps + i)),
            pl.BlockSpec((rows, width), lambda h, i: (0, (head0 + h) * steps + i)),
            pl.BlockSpec((None, ext_rows, hd), lambda h, i: (0, 0, head0 + h)),
            pl.BlockSpec((None, ext_rows, hd), lambda h, i: (1, 0, head0 + h)),
            pl.BlockSpec((None, hd, ext_rows), lambda h, i: (0, head0 + h, 0)),
            pl.BlockSpec((None, hd, ext_rows), lambda h, i: (1, head0 + h, 0)),
        ]
        + [pl.BlockSpec(memory_space=pl.ANY) for _ in after],
        out_specs=[
            pl.BlockSpec((rows, width), lambda h, i: (0, h * steps + i)),
            pl.BlockSpec((2, hd, ext_rows), lambda h, i: (0, h, 0)),
        ],
        out_shape=[
            jax.ShapeDtypeStruct((rows, heads * group * hd), jnp.bfloat16),
            jax.ShapeDtypeStruct((2, heads * hd, ext_rows), jnp.float32),
        ],
        compiler_params=pltpu.CompilerParams(dimension_semantics=("arbitrary", "arbitrary")),
        cost_estimate=pl.CostEstimate(
            flops=flops,
            transcendentals=rows * ext_rows * heads * group,
            bytes_accessed=(3 * rows * group * 2 + ext_rows * 2 * 6) * hd * heads + bias.size * 4,
        ),
    )(bias, q, g, ext, ext, ext_t, ext_t, *after)


def scatter_layers(own_rows):
    sections = lax.axis_size("section")
    peers = lax.axis_size("tp")
    kinds, rows, cols = own_rows.shape
    pieces = own_rows.reshape(kinds, peers, sections, rows // (peers * sections), cols)
    pieces = jnp.swapaxes(pieces, 1, 2).reshape(kinds, sections * peers, rows // (peers * sections), cols)
    pieces = lax.all_to_all(pieces.astype(jnp.bfloat16), ("section", "tp"), split_axis=1, concat_axis=1)
    pieces = pieces.astype(jnp.float32).reshape(kinds, sections, peers, rows // (peers * sections), cols)
    chunk = pieces[:, 0]
    for other in range(1, sections):
        chunk = chunk + pieces[:, other]
    return jnp.swapaxes(chunk, 1, 2)


def body(queries, upstream, shared_kv):
    local_kv = lax.all_to_all(shared_kv, "tp", split_axis=2, concat_axis=1, tiled=True)
    tok_rows = local_kv.shape[1]
    head_size = HD
    group_size = QH // KVH
    span_blocks = WINDOW // tok_rows
    score_scale = 1.0 / math.sqrt(head_size)
    earlier = [shifted(local_kv, "seq", span_blocks - offset) for offset in range(span_blocks)]
    extended = jnp.concatenate(earlier + [local_kv], axis=1)
    ext_rows = extended.shape[1]
    position = lax.axis_index("seq")
    row_ids = lax.broadcasted_iota(jnp.int32, (tok_rows, ext_rows), 0)
    key_ids = lax.broadcasted_iota(jnp.int32, (tok_rows, ext_rows), 1)
    allowed = (
        (key_ids >= row_ids + 1)
        & (key_ids <= row_ids + WINDOW)
        & (position * tok_rows - WINDOW + key_ids >= 0)
    )
    bias = jnp.where(allowed, 0.0, -jnp.inf).astype(jnp.float32)
    extended_t = jnp.swapaxes(extended, 1, 2)
    query_rows = queries.reshape(tok_rows, -1)
    grad_rows = upstream.reshape(tok_rows, -1)
    local_heads = extended.shape[2] // head_size
    d_query_parts = []
    own_parts = []
    sent = []
    for kv_head in range(local_heads):
        d_query_part, grad_ext = attention_grads(
            bias, query_rows, grad_rows, extended, extended_t, group_size, head_size, score_scale, 2, kv_head, 1, sent
        )
        grad_ext = jnp.swapaxes(grad_ext, 1, 2)
        d_query_parts.append(d_query_part)
        sent = [
            grad_ext[:, offset * tok_rows : (offset + 1) * tok_rows, :].astype(jnp.bfloat16)
            for offset in range(span_blocks)
        ]
        own_rows = grad_ext[:, span_blocks * tok_rows :, :]
        for offset in range(span_blocks):
            own_rows = own_rows + shifted(sent[offset], "seq", offset - span_blocks).astype(jnp.float32)
        own_parts.append(own_rows)
    d_queries = jnp.concatenate(d_query_parts, axis=1).reshape(queries.shape)
    own_rows = jnp.concatenate(own_parts, axis=2)
    chunk = scatter_layers(own_rows)
    kinds, rows, tp_peers, cols = chunk.shape
    d_shared_kv = lax.all_gather(
        chunk.reshape(kinds, rows, -1).astype(jnp.bfloat16), "section", axis=1, tiled=True
    ).astype(jnp.float32)
    return (d_queries, d_shared_kv)


def solution(mesh):
    in_specs = (P("section", "seq", "tp"), P("section", "seq", "tp"), P(None, ("seq", "tp"), None))
    out_specs = (P("section", "seq", "tp"), P(None, ("seq", "tp"), None))
    return jax.shard_map(body, mesh=mesh, in_specs=in_specs, out_specs=out_specs, check_vma=False)
```

```python
import functools
import math

import jax
import jax.numpy as jnp
from jax import lax
from jax.experimental import pallas as pl
from jax.experimental.pallas import tpu as pltpu
from jax.sharding import PartitionSpec as P

QH = 64
KVH = 8
HD = 128
WINDOW = 1024


def shifted(value, axis, by):
    peers = lax.axis_size(axis)
    pairs = [(i, i + by) for i in range(peers) if 0 <= i + by < peers]
    return lax.ppermute(value, axis, pairs)


def attn_kernel(bias_ref, q_ref, g_ref, k_ref, v_ref, *rest, scale, hd, per_step, sent_cols):
    dq_ref, dkv_ref, send_ref = rest[-3:]
    gi = pl.program_id(1)
    k = k_ref[...]
    v = v_ref[...]
    bias = bias_ref[...]
    nt = (((1,), (1,)), ((), ()))
    tn = (((0,), (0,)), ((), ()))
    dk = None
    dv = None
    for part in range(per_step):
        cols = slice(part * hd, (part + 1) * hd)
        q = q_ref[:, cols]
        do = g_ref[:, cols]
        s = lax.dot_general(q, k, nt, preferred_element_type=jnp.float32) * scale + bias
        m = jnp.max(s, axis=1, keepdims=True)
        w = jnp.exp(s - m)
        p = w * (1.0 / jnp.sum(w, axis=1, keepdims=True))
        pb = p.astype(jnp.bfloat16)
        o = jnp.dot(pb, v, preferred_element_type=jnp.float32)
        delta = jnp.sum(do.astype(jnp.float32) * o, axis=1, keepdims=True)
        dp = lax.dot_general(do, v, nt, preferred_element_type=jnp.float32)
        dsb = (p * (dp - delta)).astype(jnp.bfloat16)
        dq = jnp.dot(dsb, k, preferred_element_type=jnp.float32) * scale
        dq_ref[:, cols] = dq.astype(dq_ref.dtype)
        dk_part = lax.dot_general(q, dsb, tn, preferred_element_type=jnp.float32) * scale
        dv_part = lax.dot_general(do, pb, tn, preferred_element_type=jnp.float32)
        dk = dk_part if dk is None else dk + dk_part
        dv = dv_part if dv is None else dv + dv_part

    @pl.when(gi == 0)
    def _():
        dkv_ref[0] = dk
        dkv_ref[1] = dv

    @pl.when(gi > 0)
    def _():
        dkv_ref[0] += dk
        dkv_ref[1] += dv

    @pl.when(gi == pl.num_programs(1) - 1)
    def _():
        send_ref[0] = dkv_ref[0, :, :sent_cols].astype(send_ref.dtype)
        send_ref[1] = dkv_ref[1, :, :sent_cols].astype(send_ref.dtype)


def attention_grads(bias, q, g, ext, group, hd, scale, per_step, head0, heads, sent_cols, after=()):
    rows, _ = q.shape
    _, ext_rows, _ = ext.shape
    steps = group // per_step
    width = per_step * hd
    flops = 6 * 2 * rows * ext_rows * hd * heads * group
    return pl.pallas_call(
        functools.partial(attn_kernel, scale=scale, hd=hd, per_step=per_step, sent_cols=sent_cols),
        grid=(heads, steps),
        in_specs=[
            pl.BlockSpec((rows, ext_rows), lambda h, i: (0, 0)),
            pl.BlockSpec((rows, width), lambda h, i: (0, (head0 + h) * steps + i)),
            pl.BlockSpec((rows, width), lambda h, i: (0, (head0 + h) * steps + i)),
            pl.BlockSpec((None, ext_rows, hd), lambda h, i: (0, 0, head0 + h)),
            pl.BlockSpec((None, ext_rows, hd), lambda h, i: (1, 0, head0 + h)),
        ]
        + [pl.BlockSpec(memory_space=pl.ANY) for _ in after],
        out_specs=[
            pl.BlockSpec((rows, width), lambda h, i: (0, h * steps + i)),
            pl.BlockSpec((2, hd, ext_rows), lambda h, i: (0, h, 0)),
            pl.BlockSpec((2, hd, sent_cols), lambda h, i: (0, h, 0)),
        ],
        out_shape=[
            jax.ShapeDtypeStruct((rows, heads * group * hd), jnp.bfloat16),
            jax.ShapeDtypeStruct((2, heads * hd, ext_rows), jnp.float32),
            jax.ShapeDtypeStruct((2, heads * hd, sent_cols), jnp.bfloat16),
        ],
        compiler_params=pltpu.CompilerParams(dimension_semantics=("arbitrary", "arbitrary")),
        cost_estimate=pl.CostEstimate(
            flops=flops,
            transcendentals=rows * ext_rows * heads * group,
            bytes_accessed=(3 * rows * group * 2 + ext_rows * 2 * 6) * hd * heads + bias.size * 4,
        ),
    )(bias, q, g, ext, ext, *after)


def scatter_layers(own_rows):
    sections = lax.axis_size("section")
    peers = lax.axis_size("tp")
    kinds, rows, cols = own_rows.shape
    pieces = own_rows.reshape(kinds, peers, sections, rows // (peers * sections), cols)
    pieces = jnp.swapaxes(pieces, 1, 2).reshape(kinds, sections * peers, rows // (peers * sections), cols)
    pieces = lax.all_to_all(pieces.astype(jnp.bfloat16), ("section", "tp"), split_axis=1, concat_axis=1)
    pieces = pieces.astype(jnp.float32).reshape(kinds, sections, peers, rows // (peers * sections), cols)
    chunk = pieces[:, 0]
    for other in range(1, sections):
        chunk = chunk + pieces[:, other]
    return jnp.swapaxes(chunk, 1, 2)


def body(queries, upstream, shared_kv):
    local_kv = lax.all_to_all(shared_kv, "tp", split_axis=2, concat_axis=1, tiled=True)
    tok_rows = local_kv.shape[1]
    head_size = HD
    group_size = QH // KVH
    span_blocks = WINDOW // tok_rows
    score_scale = 1.0 / math.sqrt(head_size)
    earlier = [shifted(local_kv, "seq", span_blocks - offset) for offset in range(span_blocks)]
    extended = jnp.concatenate(earlier + [local_kv], axis=1)
    ext_rows = extended.shape[1]
    position = lax.axis_index("seq")
    row_ids = lax.broadcasted_iota(jnp.int32, (tok_rows, ext_rows), 0)
    key_ids = lax.broadcasted_iota(jnp.int32, (tok_rows, ext_rows), 1)
    allowed = (
        (key_ids >= row_ids + 1)
        & (key_ids <= row_ids + WINDOW)
        & (position * tok_rows - WINDOW + key_ids >= 0)
    )
    bias = jnp.where(allowed, 0.0, -jnp.inf).astype(jnp.float32)
    query_rows = queries.reshape(tok_rows, -1)
    grad_rows = upstream.reshape(tok_rows, -1)
    local_heads = extended.shape[2] // head_size
    d_query_parts = []
    own_parts = []
    sent = []
    for kv_head in range(local_heads):
        d_query_part, grad_t, sent_t = attention_grads(
            bias, query_rows, grad_rows, extended, group_size, head_size, score_scale, 2, kv_head, 1,
            span_blocks * tok_rows, sent,
        )
        d_query_parts.append(d_query_part)
        sent = [
            sent_t[:, :, offset * tok_rows : (offset + 1) * tok_rows]
            for offset in range(span_blocks)
        ]
        own_t = grad_t[:, :, span_blocks * tok_rows :]
        for offset in range(span_blocks):
            own_t = own_t + shifted(sent[offset], "seq", offset - span_blocks).astype(jnp.float32)
        own_parts.append(own_t)
    d_queries = jnp.concatenate(d_query_parts, axis=1).reshape(queries.shape)
    own_rows = jnp.swapaxes(jnp.concatenate(own_parts, axis=1), 1, 2)
    chunk = scatter_layers(own_rows)
    kinds, rows, tp_peers, cols = chunk.shape
    d_shared_kv = lax.all_gather(
        chunk.reshape(kinds, rows, -1).astype(jnp.bfloat16), "section", axis=1, tiled=True
    ).astype(jnp.float32)
    return (d_queries, d_shared_kv)


def solution(mesh):
    in_specs = (P("section", "seq", "tp"), P("section", "seq", "tp"), P(None, ("seq", "tp"), None))
    out_specs = (P("section", "seq", "tp"), P(None, ("seq", "tp"), None))
    return jax.shard_map(body, mesh=mesh, in_specs=in_specs, out_specs=out_specs, check_vma=False)
```

```python
import functools
import math

import jax
import jax.numpy as jnp
from jax import lax
from jax.experimental import pallas as pl
from jax.experimental.pallas import tpu as pltpu
from jax.sharding import PartitionSpec as P

QH = 64
KVH = 8
HD = 128
WINDOW = 1024


def shifted(value, axis, by):
    peers = lax.axis_size(axis)
    pairs = [(i, i + by) for i in range(peers) if 0 <= i + by < peers]
    return lax.ppermute(value, axis, pairs)


def attn_kernel(bias_ref, q_ref, g_ref, k_ref, v_ref, *rest, scale, hd, per_step, sent_cols):
    dq_ref, dkv_ref, send_ref = rest[-3:]
    gi = pl.program_id(1)
    k = k_ref[...]
    v = v_ref[...]
    bias = bias_ref[...]
    nt = (((1,), (1,)), ((), ()))
    tn = (((0,), (0,)), ((), ()))
    dk = None
    dv = None
    for part in range(per_step):
        cols = slice(part * hd, (part + 1) * hd)
        q = q_ref[:, cols]
        do = g_ref[:, cols]
        s = lax.dot_general(q, k, nt, preferred_element_type=jnp.float32) * scale + bias
        m = jnp.max(s, axis=1, keepdims=True)
        w = jnp.exp(s - m)
        p = w * (1.0 / jnp.sum(w, axis=1, keepdims=True))
        pb = p.astype(jnp.bfloat16)
        o = jnp.dot(pb, v, preferred_element_type=jnp.float32)
        delta = jnp.sum(do.astype(jnp.float32) * o, axis=1, keepdims=True)
        dp = lax.dot_general(do, v, nt, preferred_element_type=jnp.float32)
        dsb = (p * (dp - delta)).astype(jnp.bfloat16)
        dq = jnp.dot(dsb, k, preferred_element_type=jnp.float32) * scale
        dq_ref[:, cols] = dq.astype(dq_ref.dtype)
        dk_part = lax.dot_general(q, dsb, tn, preferred_element_type=jnp.float32) * scale
        dv_part = lax.dot_general(do, pb, tn, preferred_element_type=jnp.float32)
        dk = dk_part if dk is None else dk + dk_part
        dv = dv_part if dv is None else dv + dv_part

    @pl.when(gi == 0)
    def _():
        dkv_ref[0] = dk
        dkv_ref[1] = dv

    @pl.when(gi > 0)
    def _():
        dkv_ref[0] += dk
        dkv_ref[1] += dv

    @pl.when(gi == pl.num_programs(1) - 1)
    def _():
        send_ref[0] = dkv_ref[0, :, :sent_cols].astype(send_ref.dtype)
        send_ref[1] = dkv_ref[1, :, :sent_cols].astype(send_ref.dtype)


def attention_grads(bias, q, g, ext, group, hd, scale, per_step, head0, heads, sent_cols, after=()):
    rows, _ = q.shape
    _, ext_rows, _ = ext.shape
    steps = group // per_step
    width = per_step * hd
    flops = 6 * 2 * rows * ext_rows * hd * heads * group
    return pl.pallas_call(
        functools.partial(attn_kernel, scale=scale, hd=hd, per_step=per_step, sent_cols=sent_cols),
        grid=(heads, steps),
        in_specs=[
            pl.BlockSpec((rows, ext_rows), lambda h, i: (0, 0)),
            pl.BlockSpec((rows, width), lambda h, i: (0, (head0 + h) * steps + i)),
            pl.BlockSpec((rows, width), lambda h, i: (0, (head0 + h) * steps + i)),
            pl.BlockSpec((None, ext_rows, hd), lambda h, i: (0, 0, head0 + h)),
            pl.BlockSpec((None, ext_rows, hd), lambda h, i: (1, 0, head0 + h)),
        ]
        + [pl.BlockSpec(memory_space=pl.ANY) for _ in after],
        out_specs=[
            pl.BlockSpec((rows, width), lambda h, i: (0, h * steps + i)),
            pl.BlockSpec((2, hd, ext_rows), lambda h, i: (0, h, 0)),
            pl.BlockSpec((2, hd, sent_cols), lambda h, i: (0, h, 0)),
        ],
        out_shape=[
            jax.ShapeDtypeStruct((rows, heads * group * hd), jnp.bfloat16),
            jax.ShapeDtypeStruct((2, heads * hd, ext_rows), jnp.float32),
            jax.ShapeDtypeStruct((2, heads * hd, sent_cols), jnp.bfloat16),
        ],
        compiler_params=pltpu.CompilerParams(dimension_semantics=("arbitrary", "arbitrary")),
        cost_estimate=pl.CostEstimate(
            flops=flops,
            transcendentals=rows * ext_rows * heads * group,
            bytes_accessed=(3 * rows * group * 2 + ext_rows * 2 * 6) * hd * heads + bias.size * 4,
        ),
    )(bias, q, g, ext, ext, *after)


def scatter_layers(own_rows):
    sections = lax.axis_size("section")
    peers = lax.axis_size("tp")
    kinds, rows, cols = own_rows.shape
    pieces = own_rows.reshape(kinds, peers, sections, rows // (peers * sections), cols)
    pieces = jnp.swapaxes(pieces, 1, 2).reshape(kinds, sections * peers, rows // (peers * sections), cols)
    pieces = lax.all_to_all(pieces.astype(jnp.bfloat16), ("section", "tp"), split_axis=1, concat_axis=1)
    pieces = pieces.astype(jnp.float32).reshape(kinds, sections, peers, rows // (peers * sections), cols)
    chunk = pieces[:, 0]
    for other in range(1, sections):
        chunk = chunk + pieces[:, other]
    return jnp.swapaxes(chunk, 1, 2)


def body(queries, upstream, shared_kv):
    span_blocks = WINDOW // (shared_kv.shape[1] * lax.axis_size("tp"))
    earlier = [shifted(shared_kv, "seq", span_blocks - offset) for offset in range(span_blocks)]
    blocks = jnp.stack(earlier + [shared_kv], axis=1)
    blocks = lax.all_to_all(blocks, "tp", split_axis=3, concat_axis=2, tiled=True)
    kinds, _, tok_rows, kv_cols = blocks.shape
    extended = blocks.reshape(kinds, (span_blocks + 1) * tok_rows, kv_cols)
    head_size = HD
    group_size = QH // KVH
    score_scale = 1.0 / math.sqrt(head_size)
    ext_rows = extended.shape[1]
    position = lax.axis_index("seq")
    row_ids = lax.broadcasted_iota(jnp.int32, (tok_rows, ext_rows), 0)
    key_ids = lax.broadcasted_iota(jnp.int32, (tok_rows, ext_rows), 1)
    allowed = (
        (key_ids >= row_ids + 1)
        & (key_ids <= row_ids + WINDOW)
        & (position * tok_rows - WINDOW + key_ids >= 0)
    )
    bias = jnp.where(allowed, 0.0, -jnp.inf).astype(jnp.float32)
    query_rows = queries.reshape(tok_rows, -1)
    grad_rows = upstream.reshape(tok_rows, -1)
    local_heads = extended.shape[2] // head_size
    d_query_parts = []
    own_parts = []
    sent = []
    for kv_head in range(local_heads):
        d_query_part, grad_t, sent_t = attention_grads(
            bias, query_rows, grad_rows, extended, group_size, head_size, score_scale, 2, kv_head, 1,
            span_blocks * tok_rows, sent,
        )
        d_query_parts.append(d_query_part)
        sent = [
            sent_t[:, :, offset * tok_rows : (offset + 1) * tok_rows]
            for offset in range(span_blocks)
        ]
        own_t = grad_t[:, :, span_blocks * tok_rows :]
        for offset in range(span_blocks):
            own_t = own_t + shifted(sent[offset], "seq", offset - span_blocks).astype(jnp.float32)
        own_parts.append(own_t)
    d_queries = jnp.concatenate(d_query_parts, axis=1).reshape(queries.shape)
    own_rows = jnp.swapaxes(jnp.concatenate(own_parts, axis=1), 1, 2)
    chunk = scatter_layers(own_rows)
    kinds, rows, tp_peers, cols = chunk.shape
    d_shared_kv = lax.all_gather(
        chunk.reshape(kinds, rows, -1).astype(jnp.bfloat16), "section", axis=1, tiled=True
    ).astype(jnp.float32)
    return (d_queries, d_shared_kv)


def solution(mesh):
    in_specs = (P("section", "seq", "tp"), P("section", "seq", "tp"), P(None, ("seq", "tp"), None))
    out_specs = (P("section", "seq", "tp"), P(None, ("seq", "tp"), None))
    return jax.shard_map(body, mesh=mesh, in_specs=in_specs, out_specs=out_specs, check_vma=False)
```

```python
import functools
import math

import jax
import jax.numpy as jnp
from jax import lax
from jax.experimental import pallas as pl
from jax.experimental.pallas import tpu as pltpu
from jax.sharding import PartitionSpec as P

QH = 64
KVH = 8
HD = 128
WINDOW = 1024


def shifted(value, axis, by):
    peers = lax.axis_size(axis)
    pairs = [(i, i + by) for i in range(peers) if 0 <= i + by < peers]
    return lax.ppermute(value, axis, pairs)


def attn_kernel(bias_ref, q_ref, g_ref, k_ref, v_ref, *rest, scale, hd, per_step, sent_cols):
    dq_ref, dkv_ref, send_ref = rest[-3:]
    gi = pl.program_id(1)
    k = k_ref[...]
    v = v_ref[...]
    bias = bias_ref[...]
    nt = (((1,), (1,)), ((), ()))
    tn = (((0,), (0,)), ((), ()))
    dk = None
    dv = None
    for part in range(per_step):
        cols = slice(part * hd, (part + 1) * hd)
        q = q_ref[:, cols]
        do = g_ref[:, cols]
        s = lax.dot_general(q, k, nt, preferred_element_type=jnp.float32) * scale + bias
        m = jnp.max(s, axis=1, keepdims=True)
        w = jnp.exp(s - m)
        p = w * (1.0 / jnp.sum(w, axis=1, keepdims=True))
        pb = p.astype(jnp.bfloat16)
        o = jnp.dot(pb, v, preferred_element_type=jnp.float32)
        delta = jnp.sum(do.astype(jnp.float32) * o, axis=1, keepdims=True)
        dp = lax.dot_general(do, v, nt, preferred_element_type=jnp.float32)
        dsb = (p * (dp - delta)).astype(jnp.bfloat16)
        dq = jnp.dot(dsb, k, preferred_element_type=jnp.float32) * scale
        dq_ref[:, cols] = dq.astype(dq_ref.dtype)
        dk_part = lax.dot_general(q, dsb, tn, preferred_element_type=jnp.float32) * scale
        dv_part = lax.dot_general(do, pb, tn, preferred_element_type=jnp.float32)
        dk = dk_part if dk is None else dk + dk_part
        dv = dv_part if dv is None else dv + dv_part

    @pl.when(gi == 0)
    def _():
        dkv_ref[0] = dk
        dkv_ref[1] = dv

    @pl.when(gi > 0)
    def _():
        dkv_ref[0] += dk
        dkv_ref[1] += dv

    @pl.when(gi == pl.num_programs(1) - 1)
    def _():
        send_ref[0] = dkv_ref[0, :, :sent_cols].astype(send_ref.dtype)
        send_ref[1] = dkv_ref[1, :, :sent_cols].astype(send_ref.dtype)


def attention_grads(bias, q, g, ext, group, hd, scale, per_step, head0, heads, sent_cols, after=()):
    rows, _ = q.shape
    _, ext_rows, _ = ext.shape
    steps = group // per_step
    width = per_step * hd
    flops = 6 * 2 * rows * ext_rows * hd * heads * group
    return pl.pallas_call(
        functools.partial(attn_kernel, scale=scale, hd=hd, per_step=per_step, sent_cols=sent_cols),
        grid=(heads, steps),
        in_specs=[
            pl.BlockSpec((rows, ext_rows), lambda h, i: (0, 0)),
            pl.BlockSpec((rows, width), lambda h, i: (0, (head0 + h) * steps + i)),
            pl.BlockSpec((rows, width), lambda h, i: (0, (head0 + h) * steps + i)),
            pl.BlockSpec((None, ext_rows, hd), lambda h, i: (0, 0, head0 + h)),
            pl.BlockSpec((None, ext_rows, hd), lambda h, i: (1, 0, head0 + h)),
        ]
        + [pl.BlockSpec(memory_space=pl.ANY) for _ in after],
        out_specs=[
            pl.BlockSpec((rows, width), lambda h, i: (0, h * steps + i)),
            pl.BlockSpec((2, hd, ext_rows), lambda h, i: (0, h, 0)),
            pl.BlockSpec((2, hd, sent_cols), lambda h, i: (0, h, 0)),
        ],
        out_shape=[
            jax.ShapeDtypeStruct((rows, heads * group * hd), jnp.bfloat16),
            jax.ShapeDtypeStruct((2, heads * hd, ext_rows), jnp.float32),
            jax.ShapeDtypeStruct((2, heads * hd, sent_cols), jnp.bfloat16),
        ],
        compiler_params=pltpu.CompilerParams(dimension_semantics=("arbitrary", "arbitrary")),
        cost_estimate=pl.CostEstimate(
            flops=flops,
            transcendentals=rows * ext_rows * heads * group,
            bytes_accessed=(3 * rows * group * 2 + ext_rows * 2 * 6) * hd * heads + bias.size * 4,
        ),
    )(bias, q, g, ext, ext, *after)


def scatter_layers(own_rows):
    sections = lax.axis_size("section")
    peers = lax.axis_size("tp")
    kinds, rows, cols = own_rows.shape
    pieces = own_rows.reshape(kinds, peers, sections, rows // (peers * sections), cols)
    pieces = jnp.swapaxes(pieces, 1, 2).reshape(kinds, sections * peers, rows // (peers * sections), cols)
    pieces = lax.all_to_all(pieces.astype(jnp.bfloat16), ("section", "tp"), split_axis=1, concat_axis=1)
    pieces = pieces.astype(jnp.float32).reshape(kinds, sections, peers, rows // (peers * sections), cols)
    chunk = pieces[:, 0]
    for other in range(1, sections):
        chunk = chunk + pieces[:, other]
    return jnp.swapaxes(chunk, 1, 2)


def body(queries, upstream, shared_kv):
    local_kv = lax.all_to_all(shared_kv, "tp", split_axis=2, concat_axis=1, tiled=True)
    tok_rows = local_kv.shape[1]
    head_size = HD
    group_size = QH // KVH
    span_blocks = WINDOW // tok_rows
    score_scale = 1.0 / math.sqrt(head_size)
    earlier = [shifted(local_kv, "seq", span_blocks - offset) for offset in range(span_blocks)]
    extended = jnp.concatenate(earlier + [local_kv], axis=1)
    ext_rows = extended.shape[1]
    position = lax.axis_index("seq")
    row_ids = lax.broadcasted_iota(jnp.int32, (tok_rows, ext_rows), 0)
    key_ids = lax.broadcasted_iota(jnp.int32, (tok_rows, ext_rows), 1)
    allowed = (
        (key_ids >= row_ids + 1)
        & (key_ids <= row_ids + WINDOW)
        & (position * tok_rows - WINDOW + key_ids >= 0)
    )
    bias = jnp.where(allowed, 0.0, -jnp.inf).astype(jnp.float32)
    query_rows = queries.reshape(tok_rows, -1)
    grad_rows = upstream.reshape(tok_rows, -1)
    local_heads = extended.shape[2] // head_size
    d_query_rows, grad_t, sent_t = attention_grads(
        bias, query_rows, grad_rows, extended, group_size, head_size, score_scale, 2, 0, local_heads,
        span_blocks * tok_rows,
    )
    d_queries = d_query_rows.reshape(queries.shape)
    own_t = grad_t[:, :, span_blocks * tok_rows :]
    for offset in range(span_blocks):
        piece = sent_t[:, :, offset * tok_rows : (offset + 1) * tok_rows]
        own_t = own_t + shifted(piece, "seq", offset - span_blocks).astype(jnp.float32)
    own_rows = jnp.swapaxes(own_t, 1, 2)
    chunk = scatter_layers(own_rows)
    kinds, rows, tp_peers, cols = chunk.shape
    d_shared_kv = lax.all_gather(
        chunk.reshape(kinds, rows, -1).astype(jnp.bfloat16), "section", axis=1, tiled=True
    ).astype(jnp.float32)
    return (d_queries, d_shared_kv)


def solution(mesh):
    in_specs = (P("section", "seq", "tp"), P("section", "seq", "tp"), P(None, ("seq", "tp"), None))
    out_specs = (P("section", "seq", "tp"), P(None, ("seq", "tp"), None))
    return jax.shard_map(body, mesh=mesh, in_specs=in_specs, out_specs=out_specs, check_vma=False)
```

```python
import functools
import math

import jax
import jax.numpy as jnp
from jax import lax
from jax.experimental import pallas as pl
from jax.experimental.pallas import tpu as pltpu
from jax.sharding import PartitionSpec as P

QH = 64
KVH = 8
HD = 128
WINDOW = 1024


def shifted(value, axis, by):
    peers = lax.axis_size(axis)
    pairs = [(i, i + by) for i in range(peers) if 0 <= i + by < peers]
    return lax.ppermute(value, axis, pairs)


def attn_kernel(bias_ref, q_ref, g_ref, k_ref, v_ref, *rest, scale, hd, per_step, sent_cols):
    dq_ref, dkv_ref, send_ref = rest[-3:]
    gi = pl.program_id(1)
    k = k_ref[...]
    v = v_ref[...]
    bias = bias_ref[...]
    nt = (((1,), (1,)), ((), ()))
    tn = (((0,), (0,)), ((), ()))
    dk = None
    dv = None
    for part in range(per_step):
        cols = slice(part * hd, (part + 1) * hd)
        q = q_ref[:, cols]
        do = g_ref[:, cols]
        s = lax.dot_general(q, k, nt, preferred_element_type=jnp.float32) * scale + bias
        m = jnp.max(s, axis=1, keepdims=True)
        w = jnp.exp(s - m)
        p = w * (1.0 / jnp.sum(w, axis=1, keepdims=True))
        pb = p.astype(jnp.bfloat16)
        o = jnp.dot(pb, v, preferred_element_type=jnp.float32)
        delta = jnp.sum(do.astype(jnp.float32) * o, axis=1, keepdims=True)
        dp = lax.dot_general(do, v, nt, preferred_element_type=jnp.float32)
        dsb = (p * (dp - delta)).astype(jnp.bfloat16)
        dq = jnp.dot(dsb, k, preferred_element_type=jnp.float32) * scale
        dq_ref[:, cols] = dq.astype(dq_ref.dtype)
        dk_part = lax.dot_general(q, dsb, tn, preferred_element_type=jnp.float32) * scale
        dv_part = lax.dot_general(do, pb, tn, preferred_element_type=jnp.float32)
        dk = dk_part if dk is None else dk + dk_part
        dv = dv_part if dv is None else dv + dv_part

    @pl.when(gi == 0)
    def _():
        dkv_ref[0] = dk
        dkv_ref[1] = dv

    @pl.when(gi > 0)
    def _():
        dkv_ref[0] += dk
        dkv_ref[1] += dv

    @pl.when(gi == pl.num_programs(1) - 1)
    def _():
        send_ref[0] = dkv_ref[0, :, :sent_cols].astype(send_ref.dtype)
        send_ref[1] = dkv_ref[1, :, :sent_cols].astype(send_ref.dtype)


def attention_grads(bias, q, g, ext, group, hd, scale, per_step, head0, heads, sent_cols, after=()):
    rows, _ = q.shape
    _, ext_rows, _ = ext.shape
    steps = group // per_step
    width = per_step * hd
    flops = 6 * 2 * rows * ext_rows * hd * heads * group
    return pl.pallas_call(
        functools.partial(attn_kernel, scale=scale, hd=hd, per_step=per_step, sent_cols=sent_cols),
        grid=(heads, steps),
        in_specs=[
            pl.BlockSpec((rows, ext_rows), lambda h, i: (0, 0)),
            pl.BlockSpec((rows, width), lambda h, i: (0, (head0 + h) * steps + i)),
            pl.BlockSpec((rows, width), lambda h, i: (0, (head0 + h) * steps + i)),
            pl.BlockSpec((None, ext_rows, hd), lambda h, i: (0, 0, head0 + h)),
            pl.BlockSpec((None, ext_rows, hd), lambda h, i: (1, 0, head0 + h)),
        ]
        + [pl.BlockSpec(memory_space=pl.ANY) for _ in after],
        out_specs=[
            pl.BlockSpec((rows, width), lambda h, i: (0, h * steps + i)),
            pl.BlockSpec((2, hd, ext_rows), lambda h, i: (0, h, 0)),
            pl.BlockSpec((2, hd, sent_cols), lambda h, i: (0, h, 0)),
        ],
        out_shape=[
            jax.ShapeDtypeStruct((rows, heads * group * hd), jnp.bfloat16),
            jax.ShapeDtypeStruct((2, heads * hd, ext_rows), jnp.float32),
            jax.ShapeDtypeStruct((2, heads * hd, sent_cols), jnp.bfloat16),
        ],
        compiler_params=pltpu.CompilerParams(dimension_semantics=("arbitrary", "arbitrary")),
        cost_estimate=pl.CostEstimate(
            flops=flops,
            transcendentals=rows * ext_rows * heads * group,
            bytes_accessed=(3 * rows * group * 2 + ext_rows * 2 * 6) * hd * heads + bias.size * 4,
        ),
    )(bias, q, g, ext, ext, *after)


def sum_layers(own_rows):
    sections = lax.axis_size("section")
    peers = lax.axis_size("tp")
    kinds, rows, cols = own_rows.shape
    per = rows // peers
    pieces = own_rows.astype(jnp.bfloat16).reshape(kinds, 1, peers, per, cols)
    pieces = jnp.broadcast_to(pieces, (kinds, sections, peers, per, cols)).reshape(kinds, sections * peers, per, cols)
    pieces = lax.all_to_all(pieces, ("section", "tp"), split_axis=1, concat_axis=1)
    pieces = pieces.astype(jnp.float32).reshape(kinds, sections, peers, per, cols)
    total = pieces[:, 0]
    for other in range(1, sections):
        total = total + pieces[:, other]
    return jnp.swapaxes(total, 1, 2).reshape(kinds, per, peers * cols)


def body(queries, upstream, shared_kv):
    local_kv = lax.all_to_all(shared_kv, "tp", split_axis=2, concat_axis=1, tiled=True)
    tok_rows = local_kv.shape[1]
    head_size = HD
    group_size = QH // KVH
    span_blocks = WINDOW // tok_rows
    score_scale = 1.0 / math.sqrt(head_size)
    earlier = [shifted(local_kv, "seq", span_blocks - offset) for offset in range(span_blocks)]
    extended = jnp.concatenate(earlier + [local_kv], axis=1)
    ext_rows = extended.shape[1]
    position = lax.axis_index("seq")
    row_ids = lax.broadcasted_iota(jnp.int32, (tok_rows, ext_rows), 0)
    key_ids = lax.broadcasted_iota(jnp.int32, (tok_rows, ext_rows), 1)
    allowed = (
        (key_ids >= row_ids + 1)
        & (key_ids <= row_ids + WINDOW)
        & (position * tok_rows - WINDOW + key_ids >= 0)
    )
    bias = jnp.where(allowed, 0.0, -jnp.inf).astype(jnp.float32)
    query_rows = queries.reshape(tok_rows, -1)
    grad_rows = upstream.reshape(tok_rows, -1)
    local_heads = extended.shape[2] // head_size
    d_query_rows, grad_t, sent_t = attention_grads(
        bias, query_rows, grad_rows, extended, group_size, head_size, score_scale, 2, 0, local_heads,
        span_blocks * tok_rows,
    )
    d_queries = d_query_rows.reshape(queries.shape)
    own_t = grad_t[:, :, span_blocks * tok_rows :]
    for offset in range(span_blocks):
        piece = sent_t[:, :, offset * tok_rows : (offset + 1) * tok_rows]
        own_t = own_t + shifted(piece, "seq", offset - span_blocks).astype(jnp.float32)
    own_rows = jnp.swapaxes(own_t, 1, 2)
    d_shared_kv = sum_layers(own_rows)
    return (d_queries, d_shared_kv)


def solution(mesh):
    in_specs = (P("section", "seq", "tp"), P("section", "seq", "tp"), P(None, ("seq", "tp"), None))
    out_specs = (P("section", "seq", "tp"), P(None, ("seq", "tp"), None))
    return jax.shard_map(body, mesh=mesh, in_specs=in_specs, out_specs=out_specs, check_vma=False)
```

```python
import functools
import math

import jax
import jax.numpy as jnp
from jax import lax
from jax.experimental import pallas as pl
from jax.experimental.pallas import tpu as pltpu
from jax.sharding import PartitionSpec as P

QH = 64
KVH = 8
HD = 128
WINDOW = 1024


def shifted(value, axis, by):
    peers = lax.axis_size(axis)
    pairs = [(i, i + by) for i in range(peers) if 0 <= i + by < peers]
    return lax.ppermute(value, axis, pairs)


def attn_kernel(bias_ref, q_ref, g_ref, k_ref, v_ref, *rest, scale, hd, per_step, sent_cols):
    dq_ref, dkv_ref, send_ref = rest[-3:]
    gi = pl.program_id(1)
    k = k_ref[...]
    v = v_ref[...]
    bias = bias_ref[...]
    nt = (((1,), (1,)), ((), ()))
    tn = (((0,), (0,)), ((), ()))
    dk = None
    dv = None
    for part in range(per_step):
        cols = slice(part * hd, (part + 1) * hd)
        q = q_ref[:, cols]
        do = g_ref[:, cols]
        s = lax.dot_general(q, k, nt, preferred_element_type=jnp.float32) * scale + bias
        m = jnp.max(s, axis=1, keepdims=True)
        w = jnp.exp(s - m)
        p = w * (1.0 / jnp.sum(w, axis=1, keepdims=True))
        pb = p.astype(jnp.bfloat16)
        o = jnp.dot(pb, v, preferred_element_type=jnp.float32)
        delta = jnp.sum(do.astype(jnp.float32) * o, axis=1, keepdims=True)
        dp = lax.dot_general(do, v, nt, preferred_element_type=jnp.float32)
        dsb = (p * (dp - delta)).astype(jnp.bfloat16)
        dq = jnp.dot(dsb, k, preferred_element_type=jnp.float32) * scale
        dq_ref[:, cols] = dq.astype(dq_ref.dtype)
        dk_part = lax.dot_general(q, dsb, tn, preferred_element_type=jnp.float32) * scale
        dv_part = lax.dot_general(do, pb, tn, preferred_element_type=jnp.float32)
        dk = dk_part if dk is None else dk + dk_part
        dv = dv_part if dv is None else dv + dv_part

    @pl.when(gi == 0)
    def _():
        dkv_ref[0] = dk
        dkv_ref[1] = dv

    @pl.when(gi > 0)
    def _():
        dkv_ref[0] += dk
        dkv_ref[1] += dv

    @pl.when(gi == pl.num_programs(1) - 1)
    def _():
        send_ref[0] = dkv_ref[0, :, :sent_cols].astype(send_ref.dtype)
        send_ref[1] = dkv_ref[1, :, :sent_cols].astype(send_ref.dtype)


def attention_grads(bias, q, g, ext, group, hd, scale, per_step, head0, heads, sent_cols, after=()):
    rows, _ = q.shape
    _, ext_rows, _ = ext.shape
    steps = group // per_step
    width = per_step * hd
    flops = 6 * 2 * rows * ext_rows * hd * heads * group
    return pl.pallas_call(
        functools.partial(attn_kernel, scale=scale, hd=hd, per_step=per_step, sent_cols=sent_cols),
        grid=(heads, steps),
        in_specs=[
            pl.BlockSpec((rows, ext_rows), lambda h, i: (0, 0)),
            pl.BlockSpec((rows, width), lambda h, i: (0, (head0 + h) * steps + i)),
            pl.BlockSpec((rows, width), lambda h, i: (0, (head0 + h) * steps + i)),
            pl.BlockSpec((None, ext_rows, hd), lambda h, i: (0, 0, head0 + h)),
            pl.BlockSpec((None, ext_rows, hd), lambda h, i: (1, 0, head0 + h)),
        ]
        + [pl.BlockSpec(memory_space=pl.ANY) for _ in after],
        out_specs=[
            pl.BlockSpec((rows, width), lambda h, i: (0, h * steps + i)),
            pl.BlockSpec((2, hd, ext_rows), lambda h, i: (0, h, 0)),
            pl.BlockSpec((2, hd, sent_cols), lambda h, i: (0, h, 0)),
        ],
        out_shape=[
            jax.ShapeDtypeStruct((rows, heads * group * hd), jnp.bfloat16),
            jax.ShapeDtypeStruct((2, heads * hd, ext_rows), jnp.float32),
            jax.ShapeDtypeStruct((2, heads * hd, sent_cols), jnp.bfloat16),
        ],
        compiler_params=pltpu.CompilerParams(dimension_semantics=("arbitrary", "arbitrary")),
        cost_estimate=pl.CostEstimate(
            flops=flops,
            transcendentals=rows * ext_rows * heads * group,
            bytes_accessed=(3 * rows * group * 2 + ext_rows * 2 * 6) * hd * heads + bias.size * 4,
        ),
    )(bias, q, g, ext, ext, *after)


def scatter_layers(own_rows):
    sections = lax.axis_size("section")
    peers = lax.axis_size("tp")
    kinds, rows, cols = own_rows.shape
    pieces = own_rows.reshape(kinds, peers, sections, rows // (peers * sections), cols)
    pieces = jnp.swapaxes(pieces, 1, 2).reshape(kinds, sections * peers, rows // (peers * sections), cols)
    pieces = lax.all_to_all(pieces.astype(jnp.bfloat16), ("section", "tp"), split_axis=1, concat_axis=1)
    pieces = pieces.astype(jnp.float32).reshape(kinds, sections, peers, rows // (peers * sections), cols)
    chunk = pieces[:, 0]
    for other in range(1, sections):
        chunk = chunk + pieces[:, other]
    return jnp.swapaxes(chunk, 1, 2)


def body(queries, upstream, shared_kv):
    local_kv = lax.all_to_all(shared_kv, "tp", split_axis=2, concat_axis=1, tiled=True)
    tok_rows = local_kv.shape[1]
    head_size = HD
    group_size = QH // KVH
    span_blocks = WINDOW // tok_rows
    score_scale = 1.0 / math.sqrt(head_size)
    earlier = [shifted(local_kv, "seq", span_blocks - offset) for offset in range(span_blocks)]
    extended = jnp.concatenate(earlier + [local_kv], axis=1)
    ext_rows = extended.shape[1]
    position = lax.axis_index("seq")
    row_ids = lax.broadcasted_iota(jnp.int32, (tok_rows, ext_rows), 0)
    key_ids = lax.broadcasted_iota(jnp.int32, (tok_rows, ext_rows), 1)
    allowed = (
        (key_ids >= row_ids + 1)
        & (key_ids <= row_ids + WINDOW)
        & (position * tok_rows - WINDOW + key_ids >= 0)
    )
    bias = jnp.where(allowed, 0.0, -jnp.inf).astype(jnp.float32)
    query_rows = queries.reshape(tok_rows, -1)
    grad_rows = upstream.reshape(tok_rows, -1)
    local_heads = extended.shape[2] // head_size
    d_query_rows, grad_t, sent_t = attention_grads(
        bias, query_rows, grad_rows, extended, group_size, head_size, score_scale, 4, 0, local_heads,
        span_blocks * tok_rows,
    )
    d_queries = d_query_rows.reshape(queries.shape)
    own_t = grad_t[:, :, span_blocks * tok_rows :]
    for offset in range(span_blocks):
        piece = sent_t[:, :, offset * tok_rows : (offset + 1) * tok_rows]
        own_t = own_t + shifted(piece, "seq", offset - span_blocks).astype(jnp.float32)
    own_rows = jnp.swapaxes(own_t, 1, 2)
    chunk = scatter_layers(own_rows)
    kinds, rows, tp_peers, cols = chunk.shape
    d_shared_kv = lax.all_gather(
        chunk.reshape(kinds, rows, -1).astype(jnp.bfloat16), "section", axis=1, tiled=True
    ).astype(jnp.float32)
    return (d_queries, d_shared_kv)


def solution(mesh):
    in_specs = (P("section", "seq", "tp"), P("section", "seq", "tp"), P(None, ("seq", "tp"), None))
    out_specs = (P("section", "seq", "tp"), P(None, ("seq", "tp"), None))
    return jax.shard_map(body, mesh=mesh, in_specs=in_specs, out_specs=out_specs, check_vma=False)
```

```python
import functools
import math

import jax
import jax.numpy as jnp
from jax import lax
from jax.experimental import pallas as pl
from jax.experimental.pallas import tpu as pltpu
from jax.sharding import PartitionSpec as P

QH = 64
KVH = 8
HD = 128
WINDOW = 1024


def shifted(value, axis, by):
    peers = lax.axis_size(axis)
    pairs = [(i, i + by) for i in range(peers) if 0 <= i + by < peers]
    return lax.ppermute(value, axis, pairs)


def attn_kernel(bias_ref, q_ref, g_ref, k_ref, v_ref, *rest, scale, hd, per_step, sent_cols):
    dq_ref, dkv_ref, send_ref = rest[-3:]
    gi = pl.program_id(1)
    k = k_ref[...]
    v = v_ref[...]
    bias = bias_ref[...]
    nt = (((1,), (1,)), ((), ()))
    tn = (((0,), (0,)), ((), ()))
    dk = None
    dv = None
    for part in range(per_step):
        cols = slice(part * hd, (part + 1) * hd)
        q = q_ref[:, cols]
        do = g_ref[:, cols]
        s = lax.dot_general(q, k, nt, preferred_element_type=jnp.float32) * scale + bias
        m = jnp.max(s, axis=1, keepdims=True)
        w = jnp.exp(s - m)
        p = w * (1.0 / jnp.sum(w, axis=1, keepdims=True))
        pb = p.astype(jnp.bfloat16)
        o = jnp.dot(pb, v, preferred_element_type=jnp.float32)
        delta = jnp.sum(do.astype(jnp.float32) * o, axis=1, keepdims=True)
        dp = lax.dot_general(do, v, nt, preferred_element_type=jnp.float32)
        dsb = (p * (dp - delta)).astype(jnp.bfloat16)
        dq = jnp.dot(dsb, k, preferred_element_type=jnp.float32) * scale
        dq_ref[:, cols] = dq.astype(dq_ref.dtype)
        dk_part = lax.dot_general(q, dsb, tn, preferred_element_type=jnp.float32) * scale
        dv_part = lax.dot_general(do, pb, tn, preferred_element_type=jnp.float32)
        dk = dk_part if dk is None else dk + dk_part
        dv = dv_part if dv is None else dv + dv_part

    @pl.when(gi == 0)
    def _():
        dkv_ref[0] = dk
        dkv_ref[1] = dv

    @pl.when(gi > 0)
    def _():
        dkv_ref[0] += dk
        dkv_ref[1] += dv

    @pl.when(gi == pl.num_programs(1) - 1)
    def _():
        send_ref[0] = dkv_ref[0, :, :sent_cols].astype(send_ref.dtype)
        send_ref[1] = dkv_ref[1, :, :sent_cols].astype(send_ref.dtype)


def attention_grads(bias, q, g, ext, group, hd, scale, per_step, head0, heads, sent_cols, after=()):
    rows, _ = q.shape
    _, ext_rows, _ = ext.shape
    steps = group // per_step
    width = per_step * hd
    flops = 6 * 2 * rows * ext_rows * hd * heads * group
    return pl.pallas_call(
        functools.partial(attn_kernel, scale=scale, hd=hd, per_step=per_step, sent_cols=sent_cols),
        grid=(heads, steps),
        in_specs=[
            pl.BlockSpec((rows, ext_rows), lambda h, i: (0, 0)),
            pl.BlockSpec((rows, width), lambda h, i: (0, (head0 + h) * steps + i)),
            pl.BlockSpec((rows, width), lambda h, i: (0, (head0 + h) * steps + i)),
            pl.BlockSpec((None, ext_rows, hd), lambda h, i: (0, 0, head0 + h)),
            pl.BlockSpec((None, ext_rows, hd), lambda h, i: (1, 0, head0 + h)),
        ]
        + [pl.BlockSpec(memory_space=pl.ANY) for _ in after],
        out_specs=[
            pl.BlockSpec((rows, width), lambda h, i: (0, h * steps + i)),
            pl.BlockSpec((2, hd, ext_rows), lambda h, i: (0, h, 0)),
            pl.BlockSpec((2, hd, sent_cols), lambda h, i: (0, h, 0)),
        ],
        out_shape=[
            jax.ShapeDtypeStruct((rows, heads * group * hd), jnp.bfloat16),
            jax.ShapeDtypeStruct((2, heads * hd, ext_rows), jnp.float32),
            jax.ShapeDtypeStruct((2, heads * hd, sent_cols), jnp.bfloat16),
        ],
        compiler_params=pltpu.CompilerParams(dimension_semantics=("arbitrary", "arbitrary")),
        cost_estimate=pl.CostEstimate(
            flops=flops,
            transcendentals=rows * ext_rows * heads * group,
            bytes_accessed=(3 * rows * group * 2 + ext_rows * 2 * 6) * hd * heads + bias.size * 4,
        ),
    )(bias, q, g, ext, ext, *after)


def scatter_layers(own_rows):
    sections = lax.axis_size("section")
    peers = lax.axis_size("tp")
    kinds, rows, cols = own_rows.shape
    pieces = own_rows.reshape(kinds, peers, sections, rows // (peers * sections), cols)
    pieces = jnp.swapaxes(pieces, 1, 2).reshape(kinds, sections * peers, rows // (peers * sections), cols)
    pieces = lax.all_to_all(pieces.astype(jnp.bfloat16), ("section", "tp"), split_axis=1, concat_axis=1)
    pieces = pieces.astype(jnp.float32).reshape(kinds, sections, peers, rows // (peers * sections), cols)
    chunk = pieces[:, 0]
    for other in range(1, sections):
        chunk = chunk + pieces[:, other]
    return jnp.swapaxes(chunk, 1, 2)


def body(queries, upstream, shared_kv):
    local_kv = lax.all_to_all(shared_kv, "tp", split_axis=2, concat_axis=1, tiled=True)
    tok_rows = local_kv.shape[1]
    head_size = HD
    group_size = QH // KVH
    span_blocks = WINDOW // tok_rows
    score_scale = 1.0 / math.sqrt(head_size)
    earlier = [shifted(local_kv, "seq", span_blocks - offset) for offset in range(span_blocks)]
    extended = jnp.concatenate(earlier + [local_kv], axis=1)
    ext_rows = extended.shape[1]
    position = lax.axis_index("seq")
    row_ids = lax.broadcasted_iota(jnp.int32, (tok_rows, ext_rows), 0)
    key_ids = lax.broadcasted_iota(jnp.int32, (tok_rows, ext_rows), 1)
    allowed = (
        (key_ids >= row_ids + 1)
        & (key_ids <= row_ids + WINDOW)
        & (position * tok_rows - WINDOW + key_ids >= 0)
    )
    bias = jnp.where(allowed, 0.0, -jnp.inf).astype(jnp.float32)
    query_rows = queries.reshape(tok_rows, -1)
    grad_rows = upstream.reshape(tok_rows, -1)
    local_heads = extended.shape[2] // head_size
    d_query_rows, grad_t, sent_t = attention_grads(
        bias, query_rows, grad_rows, extended, group_size, head_size, score_scale, group_size, 0, local_heads,
        span_blocks * tok_rows,
    )
    d_queries = d_query_rows.reshape(queries.shape)
    own_t = grad_t[:, :, span_blocks * tok_rows :]
    for offset in range(span_blocks):
        piece = sent_t[:, :, offset * tok_rows : (offset + 1) * tok_rows]
        own_t = own_t + shifted(piece, "seq", offset - span_blocks).astype(jnp.float32)
    own_rows = jnp.swapaxes(own_t, 1, 2)
    chunk = scatter_layers(own_rows)
    kinds, rows, tp_peers, cols = chunk.shape
    d_shared_kv = lax.all_gather(
        chunk.reshape(kinds, rows, -1).astype(jnp.bfloat16), "section", axis=1, tiled=True
    ).astype(jnp.float32)
    return (d_queries, d_shared_kv)


def solution(mesh):
    in_specs = (P("section", "seq", "tp"), P("section", "seq", "tp"), P(None, ("seq", "tp"), None))
    out_specs = (P("section", "seq", "tp"), P(None, ("seq", "tp"), None))
    return jax.shard_map(body, mesh=mesh, in_specs=in_specs, out_specs=out_specs, check_vma=False)
```

```python
import functools
import math

import jax
import jax.numpy as jnp
from jax import lax
from jax.experimental import pallas as pl
from jax.experimental.pallas import tpu as pltpu
from jax.sharding import PartitionSpec as P

QH = 64
KVH = 8
HD = 128
WINDOW = 1024


def shifted(value, axis, by):
    peers = lax.axis_size(axis)
    pairs = [(i, i + by) for i in range(peers) if 0 <= i + by < peers]
    return lax.ppermute(value, axis, pairs)


def attn_kernel(bias_ref, q_ref, g_ref, k_ref, v_ref, *rest, scale, hd, per_step, sent_cols):
    dq_ref, own_ref, send_ref = rest[-3:]
    k = k_ref[...]
    v = v_ref[...]
    bias = bias_ref[...]
    nt = (((1,), (1,)), ((), ()))
    tn = (((0,), (0,)), ((), ()))
    dk = None
    dv = None
    for part in range(per_step):
        cols = slice(part * hd, (part + 1) * hd)
        q = q_ref[:, cols]
        do = g_ref[:, cols]
        s = lax.dot_general(q, k, nt, preferred_element_type=jnp.float32) * scale + bias
        m = jnp.max(s, axis=1, keepdims=True)
        w = jnp.exp(s - m)
        p = w * (1.0 / jnp.sum(w, axis=1, keepdims=True))
        pb = p.astype(jnp.bfloat16)
        o = jnp.dot(pb, v, preferred_element_type=jnp.float32)
        delta = jnp.sum(do.astype(jnp.float32) * o, axis=1, keepdims=True)
        dp = lax.dot_general(do, v, nt, preferred_element_type=jnp.float32)
        dsb = (p * (dp - delta)).astype(jnp.bfloat16)
        dq = jnp.dot(dsb, k, preferred_element_type=jnp.float32) * scale
        dq_ref[:, cols] = dq.astype(dq_ref.dtype)
        dk_part = lax.dot_general(q, dsb, tn, preferred_element_type=jnp.float32) * scale
        dv_part = lax.dot_general(do, pb, tn, preferred_element_type=jnp.float32)
        dk = dk_part if dk is None else dk + dk_part
        dv = dv_part if dv is None else dv + dv_part

    own_ref[0] = dk[:, sent_cols:]
    own_ref[1] = dv[:, sent_cols:]
    send_ref[0] = dk[:, :sent_cols].astype(send_ref.dtype)
    send_ref[1] = dv[:, :sent_cols].astype(send_ref.dtype)


def attention_grads(bias, q, g, ext, group, hd, scale, per_step, head0, heads, sent_cols, after=()):
    rows, _ = q.shape
    _, ext_rows, _ = ext.shape
    steps = group // per_step
    assert steps == 1
    width = per_step * hd
    flops = 6 * 2 * rows * ext_rows * hd * heads * group
    return pl.pallas_call(
        functools.partial(attn_kernel, scale=scale, hd=hd, per_step=per_step, sent_cols=sent_cols),
        grid=(heads, steps),
        in_specs=[
            pl.BlockSpec((rows, ext_rows), lambda h, i: (0, 0)),
            pl.BlockSpec((rows, width), lambda h, i: (0, (head0 + h) * steps + i)),
            pl.BlockSpec((rows, width), lambda h, i: (0, (head0 + h) * steps + i)),
            pl.BlockSpec((None, ext_rows, hd), lambda h, i: (0, 0, head0 + h)),
            pl.BlockSpec((None, ext_rows, hd), lambda h, i: (1, 0, head0 + h)),
        ]
        + [pl.BlockSpec(memory_space=pl.ANY) for _ in after],
        out_specs=[
            pl.BlockSpec((rows, width), lambda h, i: (0, h * steps + i)),
            pl.BlockSpec((2, hd, ext_rows - sent_cols), lambda h, i: (0, h, 0)),
            pl.BlockSpec((2, hd, sent_cols), lambda h, i: (0, h, 0)),
        ],
        out_shape=[
            jax.ShapeDtypeStruct((rows, heads * group * hd), jnp.bfloat16),
            jax.ShapeDtypeStruct((2, heads * hd, ext_rows - sent_cols), jnp.float32),
            jax.ShapeDtypeStruct((2, heads * hd, sent_cols), jnp.bfloat16),
        ],
        compiler_params=pltpu.CompilerParams(dimension_semantics=("arbitrary", "arbitrary")),
        cost_estimate=pl.CostEstimate(
            flops=flops,
            transcendentals=rows * ext_rows * heads * group,
            bytes_accessed=(3 * rows * group * 2 + ext_rows * 2 * 6) * hd * heads + bias.size * 4,
        ),
    )(bias, q, g, ext, ext, *after)


def scatter_layers(own_rows):
    sections = lax.axis_size("section")
    peers = lax.axis_size("tp")
    kinds, rows, cols = own_rows.shape
    pieces = own_rows.reshape(kinds, peers, sections, rows // (peers * sections), cols)
    pieces = jnp.swapaxes(pieces, 1, 2).reshape(kinds, sections * peers, rows // (peers * sections), cols)
    pieces = lax.all_to_all(pieces.astype(jnp.bfloat16), ("section", "tp"), split_axis=1, concat_axis=1)
    pieces = pieces.astype(jnp.float32).reshape(kinds, sections, peers, rows // (peers * sections), cols)
    chunk = pieces[:, 0]
    for other in range(1, sections):
        chunk = chunk + pieces[:, other]
    return jnp.swapaxes(chunk, 1, 2)


def body(queries, upstream, shared_kv):
    local_kv = lax.all_to_all(shared_kv, "tp", split_axis=2, concat_axis=1, tiled=True)
    tok_rows = local_kv.shape[1]
    head_size = HD
    group_size = QH // KVH
    span_blocks = WINDOW // tok_rows
    score_scale = 1.0 / math.sqrt(head_size)
    earlier = [shifted(local_kv, "seq", span_blocks - offset) for offset in range(span_blocks)]
    extended = jnp.concatenate(earlier + [local_kv], axis=1)
    ext_rows = extended.shape[1]
    position = lax.axis_index("seq")
    row_ids = lax.broadcasted_iota(jnp.int32, (tok_rows, ext_rows), 0)
    key_ids = lax.broadcasted_iota(jnp.int32, (tok_rows, ext_rows), 1)
    allowed = (
        (key_ids >= row_ids + 1)
        & (key_ids <= row_ids + WINDOW)
        & (position * tok_rows - WINDOW + key_ids >= 0)
    )
    bias = jnp.where(allowed, 0.0, -jnp.inf).astype(jnp.float32)
    query_rows = queries.reshape(tok_rows, -1)
    grad_rows = upstream.reshape(tok_rows, -1)
    local_heads = extended.shape[2] // head_size
    d_query_rows, grad_t, sent_t = attention_grads(
        bias, query_rows, grad_rows, extended, group_size, head_size, score_scale, group_size, 0, local_heads,
        span_blocks * tok_rows,
    )
    d_queries = d_query_rows.reshape(queries.shape)
    own_t = grad_t
    for offset in range(span_blocks):
        piece = sent_t[:, :, offset * tok_rows : (offset + 1) * tok_rows]
        own_t = own_t + shifted(piece, "seq", offset - span_blocks).astype(jnp.float32)
    own_rows = jnp.swapaxes(own_t, 1, 2)
    chunk = scatter_layers(own_rows)
    kinds, rows, tp_peers, cols = chunk.shape
    d_shared_kv = lax.all_gather(
        chunk.reshape(kinds, rows, -1).astype(jnp.bfloat16), "section", axis=1, tiled=True
    ).astype(jnp.float32)
    return (d_queries, d_shared_kv)


def solution(mesh):
    in_specs = (P("section", "seq", "tp"), P("section", "seq", "tp"), P(None, ("seq", "tp"), None))
    out_specs = (P("section", "seq", "tp"), P(None, ("seq", "tp"), None))
    return jax.shard_map(body, mesh=mesh, in_specs=in_specs, out_specs=out_specs, check_vma=False)
```

```python
import functools
import math

import jax
import jax.numpy as jnp
from jax import lax
from jax.experimental import pallas as pl
from jax.experimental.pallas import tpu as pltpu
from jax.sharding import PartitionSpec as P

QH = 64
KVH = 8
HD = 128
WINDOW = 1024


def shifted(value, axis, by):
    peers = lax.axis_size(axis)
    pairs = [(i, i + by) for i in range(peers) if 0 <= i + by < peers]
    return lax.ppermute(value, axis, pairs)


def attn_kernel(bias_ref, q_ref, g_ref, k_ref, v_ref, *rest, scale, hd, per_step, sent_cols):
    dq_ref, own_ref, send_ref = rest[-3:]
    k = k_ref[...]
    v = v_ref[...]
    bias = bias_ref[...]
    nt = (((1,), (1,)), ((), ()))
    tn = (((0,), (0,)), ((), ()))
    dk = None
    dv = None
    for part in range(per_step):
        cols = slice(part * hd, (part + 1) * hd)
        q = q_ref[:, cols]
        do = g_ref[:, cols]
        s = lax.dot_general(q, k, nt, preferred_element_type=jnp.float32) * scale + bias
        m = jnp.max(s, axis=1, keepdims=True)
        w = jnp.exp(s - m)
        p = w * (1.0 / jnp.sum(w, axis=1, keepdims=True))
        pb = p.astype(jnp.bfloat16)
        o = jnp.dot(pb, v, preferred_element_type=jnp.float32)
        delta = jnp.sum(do.astype(jnp.float32) * o, axis=1, keepdims=True)
        dp = lax.dot_general(do, v, nt, preferred_element_type=jnp.float32)
        dsb = (p * (dp - delta)).astype(jnp.bfloat16)
        dq = jnp.dot(dsb, k, preferred_element_type=jnp.float32) * scale
        dq_ref[:, cols] = dq.astype(dq_ref.dtype)
        dk_part = lax.dot_general(q, dsb, tn, preferred_element_type=jnp.float32) * scale
        dv_part = lax.dot_general(do, pb, tn, preferred_element_type=jnp.float32)
        dk = dk_part if dk is None else dk + dk_part
        dv = dv_part if dv is None else dv + dv_part

    own_ref[0] = dk[:, sent_cols:]
    own_ref[1] = dv[:, sent_cols:]
    piece = send_ref.shape[-1]
    for offset in range(send_ref.shape[0]):
        lanes = slice(offset * piece, (offset + 1) * piece)
        send_ref[offset, 0] = dk[:, lanes].astype(send_ref.dtype)
        send_ref[offset, 1] = dv[:, lanes].astype(send_ref.dtype)


def attention_grads(bias, q, g, ext, group, hd, scale, per_step, head0, heads, sent_cols, piece, after=()):
    rows, _ = q.shape
    _, ext_rows, _ = ext.shape
    steps = group // per_step
    assert steps == 1
    width = per_step * hd
    flops = 6 * 2 * rows * ext_rows * hd * heads * group
    return pl.pallas_call(
        functools.partial(attn_kernel, scale=scale, hd=hd, per_step=per_step, sent_cols=sent_cols),
        grid=(heads, steps),
        in_specs=[
            pl.BlockSpec((rows, ext_rows), lambda h, i: (0, 0)),
            pl.BlockSpec((rows, width), lambda h, i: (0, (head0 + h) * steps + i)),
            pl.BlockSpec((rows, width), lambda h, i: (0, (head0 + h) * steps + i)),
            pl.BlockSpec((None, ext_rows, hd), lambda h, i: (0, 0, head0 + h)),
            pl.BlockSpec((None, ext_rows, hd), lambda h, i: (1, 0, head0 + h)),
        ]
        + [pl.BlockSpec(memory_space=pl.ANY) for _ in after],
        out_specs=[
            pl.BlockSpec((rows, width), lambda h, i: (0, h * steps + i)),
            pl.BlockSpec((2, hd, ext_rows - sent_cols), lambda h, i: (0, h, 0)),
            pl.BlockSpec((sent_cols // piece, 2, hd, piece), lambda h, i: (0, 0, h, 0)),
        ],
        out_shape=[
            jax.ShapeDtypeStruct((rows, heads * group * hd), jnp.bfloat16),
            jax.ShapeDtypeStruct((2, heads * hd, ext_rows - sent_cols), jnp.float32),
            jax.ShapeDtypeStruct((sent_cols // piece, 2, heads * hd, piece), jnp.bfloat16),
        ],
        compiler_params=pltpu.CompilerParams(dimension_semantics=("arbitrary", "arbitrary")),
        cost_estimate=pl.CostEstimate(
            flops=flops,
            transcendentals=rows * ext_rows * heads * group,
            bytes_accessed=(3 * rows * group * 2 + ext_rows * 2 * 6) * hd * heads + bias.size * 4,
        ),
    )(bias, q, g, ext, ext, *after)


def scatter_layers(own_rows):
    sections = lax.axis_size("section")
    peers = lax.axis_size("tp")
    kinds, rows, cols = own_rows.shape
    pieces = own_rows.reshape(kinds, peers, sections, rows // (peers * sections), cols)
    pieces = jnp.swapaxes(pieces, 1, 2).reshape(kinds, sections * peers, rows // (peers * sections), cols)
    pieces = lax.all_to_all(pieces.astype(jnp.bfloat16), ("section", "tp"), split_axis=1, concat_axis=1)
    pieces = pieces.astype(jnp.float32).reshape(kinds, sections, peers, rows // (peers * sections), cols)
    chunk = pieces[:, 0]
    for other in range(1, sections):
        chunk = chunk + pieces[:, other]
    return jnp.swapaxes(chunk, 1, 2)


def body(queries, upstream, shared_kv):
    local_kv = lax.all_to_all(shared_kv, "tp", split_axis=2, concat_axis=1, tiled=True)
    tok_rows = local_kv.shape[1]
    head_size = HD
    group_size = QH // KVH
    span_blocks = WINDOW // tok_rows
    score_scale = 1.0 / math.sqrt(head_size)
    earlier = [shifted(local_kv, "seq", span_blocks - offset) for offset in range(span_blocks)]
    extended = jnp.concatenate(earlier + [local_kv], axis=1)
    ext_rows = extended.shape[1]
    position = lax.axis_index("seq")
    row_ids = lax.broadcasted_iota(jnp.int32, (tok_rows, ext_rows), 0)
    key_ids = lax.broadcasted_iota(jnp.int32, (tok_rows, ext_rows), 1)
    allowed = (
        (key_ids >= row_ids + 1)
        & (key_ids <= row_ids + WINDOW)
        & (position * tok_rows - WINDOW + key_ids >= 0)
    )
    bias = jnp.where(allowed, 0.0, -jnp.inf).astype(jnp.float32)
    query_rows = queries.reshape(tok_rows, -1)
    grad_rows = upstream.reshape(tok_rows, -1)
    local_heads = extended.shape[2] // head_size
    d_query_rows, grad_t, sent_t = attention_grads(
        bias, query_rows, grad_rows, extended, group_size, head_size, score_scale, group_size, 0, local_heads,
        span_blocks * tok_rows, tok_rows,
    )
    d_queries = d_query_rows.reshape(queries.shape)
    own_t = grad_t
    for offset in range(span_blocks):
        piece = sent_t[offset]
        own_t = own_t + shifted(piece, "seq", offset - span_blocks).astype(jnp.float32)
    own_rows = jnp.swapaxes(own_t, 1, 2)
    chunk = scatter_layers(own_rows)
    kinds, rows, tp_peers, cols = chunk.shape
    d_shared_kv = lax.all_gather(
        chunk.reshape(kinds, rows, -1).astype(jnp.bfloat16), "section", axis=1, tiled=True
    ).astype(jnp.float32)
    return (d_queries, d_shared_kv)


def solution(mesh):
    in_specs = (P("section", "seq", "tp"), P("section", "seq", "tp"), P(None, ("seq", "tp"), None))
    out_specs = (P("section", "seq", "tp"), P(None, ("seq", "tp"), None))
    return jax.shard_map(body, mesh=mesh, in_specs=in_specs, out_specs=out_specs, check_vma=False)
```

```python
import functools
import math

import jax
import jax.numpy as jnp
from jax import lax
from jax.experimental import pallas as pl
from jax.experimental.pallas import tpu as pltpu
from jax.sharding import PartitionSpec as P

QH = 64
KVH = 8
HD = 128
WINDOW = 1024


def shifted(value, axis, by):
    peers = lax.axis_size(axis)
    pairs = [(i, i + by) for i in range(peers) if 0 <= i + by < peers]
    return lax.ppermute(value, axis, pairs)


def attn_kernel(bias_ref, q_ref, g_ref, k_ref, v_ref, *rest, scale, hd, per_step, sent_cols, window):
    dq_ref, own_ref, send_ref = rest[-3:]
    k = k_ref[...]
    v = v_ref[...]
    lines = lax.broadcasted_iota(jnp.int32, (q_ref.shape[0], k_ref.shape[0]), 0)
    keys = lax.broadcasted_iota(jnp.int32, (q_ref.shape[0], k_ref.shape[0]), 1)
    allowed = (
        (keys >= lines + 1)
        & (keys <= lines + window)
        & (bias_ref[0] * q_ref.shape[0] - window + keys >= 0)
    )
    bias = jnp.where(allowed, 0.0, -jnp.inf).astype(jnp.float32)
    nt = (((1,), (1,)), ((), ()))
    tn = (((0,), (0,)), ((), ()))
    dk = None
    dv = None
    for part in range(per_step):
        cols = slice(part * hd, (part + 1) * hd)
        q = q_ref[:, cols]
        do = g_ref[:, cols]
        s = lax.dot_general(q, k, nt, preferred_element_type=jnp.float32) * scale + bias
        m = jnp.max(s, axis=1, keepdims=True)
        w = jnp.exp(s - m)
        p = w * (1.0 / jnp.sum(w, axis=1, keepdims=True))
        pb = p.astype(jnp.bfloat16)
        o = jnp.dot(pb, v, preferred_element_type=jnp.float32)
        delta = jnp.sum(do.astype(jnp.float32) * o, axis=1, keepdims=True)
        dp = lax.dot_general(do, v, nt, preferred_element_type=jnp.float32)
        dsb = (p * (dp - delta)).astype(jnp.bfloat16)
        dq = jnp.dot(dsb, k, preferred_element_type=jnp.float32) * scale
        dq_ref[:, cols] = dq.astype(dq_ref.dtype)
        dk_part = lax.dot_general(q, dsb, tn, preferred_element_type=jnp.float32) * scale
        dv_part = lax.dot_general(do, pb, tn, preferred_element_type=jnp.float32)
        dk = dk_part if dk is None else dk + dk_part
        dv = dv_part if dv is None else dv + dv_part

    own_ref[0] = dk[:, sent_cols:]
    own_ref[1] = dv[:, sent_cols:]
    send_ref[0] = dk[:, :sent_cols].astype(send_ref.dtype)
    send_ref[1] = dv[:, :sent_cols].astype(send_ref.dtype)


def attention_grads(bias, q, g, ext, group, hd, scale, per_step, head0, heads, sent_cols, after=()):
    rows, _ = q.shape
    _, ext_rows, _ = ext.shape
    steps = group // per_step
    assert steps == 1
    width = per_step * hd
    flops = 6 * 2 * rows * ext_rows * hd * heads * group
    return pl.pallas_call(
        functools.partial(attn_kernel, scale=scale, hd=hd, per_step=per_step, sent_cols=sent_cols, window=WINDOW),
        grid=(heads, steps),
        in_specs=[
            pl.BlockSpec(memory_space=pltpu.SMEM),
            pl.BlockSpec((rows, width), lambda h, i: (0, (head0 + h) * steps + i)),
            pl.BlockSpec((rows, width), lambda h, i: (0, (head0 + h) * steps + i)),
            pl.BlockSpec((None, ext_rows, hd), lambda h, i: (0, 0, head0 + h)),
            pl.BlockSpec((None, ext_rows, hd), lambda h, i: (1, 0, head0 + h)),
        ]
        + [pl.BlockSpec(memory_space=pl.ANY) for _ in after],
        out_specs=[
            pl.BlockSpec((rows, width), lambda h, i: (0, h * steps + i)),
            pl.BlockSpec((2, hd, ext_rows - sent_cols), lambda h, i: (0, h, 0)),
            pl.BlockSpec((2, hd, sent_cols), lambda h, i: (0, h, 0)),
        ],
        out_shape=[
            jax.ShapeDtypeStruct((rows, heads * group * hd), jnp.bfloat16),
            jax.ShapeDtypeStruct((2, heads * hd, ext_rows - sent_cols), jnp.float32),
            jax.ShapeDtypeStruct((2, heads * hd, sent_cols), jnp.bfloat16),
        ],
        compiler_params=pltpu.CompilerParams(dimension_semantics=("arbitrary", "arbitrary")),
        cost_estimate=pl.CostEstimate(
            flops=flops,
            transcendentals=rows * ext_rows * heads * group,
            bytes_accessed=(3 * rows * group * 2 + ext_rows * 2 * 6) * hd * heads,
        ),
    )(bias, q, g, ext, ext, *after)


def scatter_layers(own_rows):
    sections = lax.axis_size("section")
    peers = lax.axis_size("tp")
    kinds, rows, cols = own_rows.shape
    pieces = own_rows.reshape(kinds, peers, sections, rows // (peers * sections), cols)
    pieces = jnp.swapaxes(pieces, 1, 2).reshape(kinds, sections * peers, rows // (peers * sections), cols)
    pieces = lax.all_to_all(pieces.astype(jnp.bfloat16), ("section", "tp"), split_axis=1, concat_axis=1)
    pieces = pieces.astype(jnp.float32).reshape(kinds, sections, peers, rows // (peers * sections), cols)
    chunk = pieces[:, 0]
    for other in range(1, sections):
        chunk = chunk + pieces[:, other]
    return jnp.swapaxes(chunk, 1, 2)


def body(queries, upstream, shared_kv):
    local_kv = lax.all_to_all(shared_kv, "tp", split_axis=2, concat_axis=1, tiled=True)
    tok_rows = local_kv.shape[1]
    head_size = HD
    group_size = QH // KVH
    span_blocks = WINDOW // tok_rows
    score_scale = 1.0 / math.sqrt(head_size)
    earlier = [shifted(local_kv, "seq", span_blocks - offset) for offset in range(span_blocks)]
    extended = jnp.concatenate(earlier + [local_kv], axis=1)
    ext_rows = extended.shape[1]
    position = lax.axis_index("seq")
    row_ids = lax.broadcasted_iota(jnp.int32, (tok_rows, ext_rows), 0)
    key_ids = lax.broadcasted_iota(jnp.int32, (tok_rows, ext_rows), 1)
    allowed = (
        (key_ids >= row_ids + 1)
        & (key_ids <= row_ids + WINDOW)
        & (position * tok_rows - WINDOW + key_ids >= 0)
    )
    bias = jnp.reshape(position, (1,)).astype(jnp.int32)
    query_rows = queries.reshape(tok_rows, -1)
    grad_rows = upstream.reshape(tok_rows, -1)
    local_heads = extended.shape[2] // head_size
    d_query_rows, grad_t, sent_t = attention_grads(
        bias, query_rows, grad_rows, extended, group_size, head_size, score_scale, group_size, 0, local_heads,
        span_blocks * tok_rows,
    )
    d_queries = d_query_rows.reshape(queries.shape)
    own_t = grad_t
    for offset in range(span_blocks):
        piece = sent_t[:, :, offset * tok_rows : (offset + 1) * tok_rows]
        own_t = own_t + shifted(piece, "seq", offset - span_blocks).astype(jnp.float32)
    own_rows = jnp.swapaxes(own_t, 1, 2)
    chunk = scatter_layers(own_rows)
    kinds, rows, tp_peers, cols = chunk.shape
    d_shared_kv = lax.all_gather(
        chunk.reshape(kinds, rows, -1).astype(jnp.bfloat16), "section", axis=1, tiled=True
    ).astype(jnp.float32)
    return (d_queries, d_shared_kv)


def solution(mesh):
    in_specs = (P("section", "seq", "tp"), P("section", "seq", "tp"), P(None, ("seq", "tp"), None))
    out_specs = (P("section", "seq", "tp"), P(None, ("seq", "tp"), None))
    return jax.shard_map(body, mesh=mesh, in_specs=in_specs, out_specs=out_specs, check_vma=False)
```

```python
import functools
import math

import jax
import jax.numpy as jnp
from jax import lax
from jax.experimental import pallas as pl
from jax.experimental.pallas import tpu as pltpu
from jax.sharding import PartitionSpec as P

QH = 64
KVH = 8
HD = 128
WINDOW = 1024


def shifted(value, axis, by):
    peers = lax.axis_size(axis)
    pairs = [(i, i + by) for i in range(peers) if 0 <= i + by < peers]
    return lax.ppermute(value, axis, pairs)


def attn_kernel(bias_ref, q_ref, g_ref, k_ref, v_ref, *rest, scale, hd, per_step, sent_cols, window):
    dq_ref, own_ref, send_ref = rest[-3:]
    k = k_ref[...]
    v = v_ref[...]
    lines = lax.broadcasted_iota(jnp.int32, (q_ref.shape[0], k_ref.shape[0]), 0)
    keys = lax.broadcasted_iota(jnp.int32, (q_ref.shape[0], k_ref.shape[0]), 1)
    allowed = (
        (keys >= lines + 1)
        & (keys <= lines + window)
        & (bias_ref[0] * q_ref.shape[0] - window + keys >= 0)
    )
    bias = jnp.where(allowed, 0.0, -jnp.inf).astype(jnp.float32)
    nt = (((1,), (1,)), ((), ()))
    tn = (((0,), (0,)), ((), ()))
    dk = None
    dv = None
    for part in range(per_step):
        cols = slice(part * hd, (part + 1) * hd)
        q = q_ref[:, cols]
        do = g_ref[:, cols]
        s = lax.dot_general(q, k, nt, preferred_element_type=jnp.float32) * scale + bias
        m = jnp.max(s, axis=1, keepdims=True)
        w = jnp.exp(s - m)
        p = w * (1.0 / jnp.sum(w, axis=1, keepdims=True))
        pb = p.astype(jnp.bfloat16)
        o = jnp.dot(pb, v, preferred_element_type=jnp.float32)
        delta = jnp.sum(do.astype(jnp.float32) * o, axis=1, keepdims=True)
        dp = lax.dot_general(do, v, nt, preferred_element_type=jnp.float32)
        dsb = (p * (dp - delta)).astype(jnp.bfloat16)
        dq = jnp.dot(dsb, k, preferred_element_type=jnp.float32) * scale
        dq_ref[:, cols] = dq.astype(dq_ref.dtype)
        dk_part = lax.dot_general(q, dsb, tn, preferred_element_type=jnp.float32) * scale
        dv_part = lax.dot_general(do, pb, tn, preferred_element_type=jnp.float32)
        dk = dk_part if dk is None else dk + dk_part
        dv = dv_part if dv is None else dv + dv_part

    own_ref[0] = dk[:, sent_cols:]
    own_ref[1] = dv[:, sent_cols:]
    send_ref[0] = dk[:, :sent_cols].astype(send_ref.dtype)
    send_ref[1] = dv[:, :sent_cols].astype(send_ref.dtype)


def attention_grads(bias, q, g, ext, group, hd, scale, per_step, head0, heads, sent_cols, after=()):
    rows, _ = q.shape
    _, ext_rows, _ = ext.shape
    steps = group // per_step
    assert steps == 1
    width = per_step * hd
    flops = 6 * 2 * rows * ext_rows * hd * heads * group
    return pl.pallas_call(
        functools.partial(attn_kernel, scale=scale, hd=hd, per_step=per_step, sent_cols=sent_cols, window=WINDOW),
        grid=(heads, steps),
        in_specs=[
            pl.BlockSpec(memory_space=pltpu.SMEM),
            pl.BlockSpec((rows, width), lambda h, i: (0, (head0 + h) * steps + i)),
            pl.BlockSpec((rows, width), lambda h, i: (0, (head0 + h) * steps + i)),
            pl.BlockSpec((None, ext_rows, hd), lambda h, i: (0, 0, head0 + h)),
            pl.BlockSpec((None, ext_rows, hd), lambda h, i: (1, 0, head0 + h)),
        ]
        + [pl.BlockSpec(memory_space=pl.ANY) for _ in after],
        out_specs=[
            pl.BlockSpec((rows, width), lambda h, i: (0, h * steps + i)),
            pl.BlockSpec((2, hd, ext_rows - sent_cols), lambda h, i: (0, h, 0)),
            pl.BlockSpec((2, hd, sent_cols), lambda h, i: (0, h, 0)),
        ],
        out_shape=[
            jax.ShapeDtypeStruct((rows, heads * group * hd), jnp.bfloat16),
            jax.ShapeDtypeStruct((2, heads * hd, ext_rows - sent_cols), jnp.float32),
            jax.ShapeDtypeStruct((2, heads * hd, sent_cols), jnp.bfloat16),
        ],
        compiler_params=pltpu.CompilerParams(dimension_semantics=("arbitrary", "arbitrary")),
        cost_estimate=pl.CostEstimate(
            flops=flops,
            transcendentals=rows * ext_rows * heads * group,
            bytes_accessed=(3 * rows * group * 2 + ext_rows * 2 * 6) * hd * heads,
        ),
    )(bias, q, g, ext, ext, *after)


def scatter_layers(own_rows):
    sections = lax.axis_size("section")
    peers = lax.axis_size("tp")
    kinds, rows, cols = own_rows.shape
    pieces = own_rows.reshape(kinds, peers, sections, rows // (peers * sections), cols)
    pieces = jnp.swapaxes(pieces, 1, 2).reshape(kinds, sections * peers, rows // (peers * sections), cols)
    pieces = lax.all_to_all(pieces.astype(jnp.bfloat16), ("section", "tp"), split_axis=1, concat_axis=1)
    pieces = pieces.astype(jnp.float32).reshape(kinds, sections, peers, rows // (peers * sections), cols)
    chunk = pieces[:, 0]
    for other in range(1, sections):
        chunk = chunk + pieces[:, other]
    return jnp.swapaxes(chunk, 1, 2)


def body(queries, upstream, shared_kv):
    local_kv = lax.all_to_all(shared_kv, "tp", split_axis=2, concat_axis=1, tiled=True)
    tok_rows = local_kv.shape[1]
    head_size = HD
    group_size = QH // KVH
    span_blocks = WINDOW // tok_rows
    score_scale = 1.0 / math.sqrt(head_size)
    earlier = [shifted(local_kv, "seq", span_blocks - offset) for offset in range(span_blocks)]
    extended = jnp.concatenate(earlier + [local_kv], axis=1)
    ext_rows = extended.shape[1]
    position = lax.axis_index("seq")
    row_ids = lax.broadcasted_iota(jnp.int32, (tok_rows, ext_rows), 0)
    key_ids = lax.broadcasted_iota(jnp.int32, (tok_rows, ext_rows), 1)
    allowed = (
        (key_ids >= row_ids + 1)
        & (key_ids <= row_ids + WINDOW)
        & (position * tok_rows - WINDOW + key_ids >= 0)
    )
    bias = jnp.reshape(position, (1,)).astype(jnp.int32)
    query_rows = queries.reshape(tok_rows, -1)
    grad_rows = upstream.reshape(tok_rows, -1)
    local_heads = extended.shape[2] // head_size
    d_query_rows, grad_t, sent_t = attention_grads(
        bias, query_rows, grad_rows, extended, group_size, head_size, score_scale, group_size, 0, local_heads,
        span_blocks * tok_rows,
    )
    d_queries = d_query_rows.reshape(queries.shape)
    own_t = grad_t
    for offset in range(span_blocks):
        piece = sent_t[:, :, offset * tok_rows : (offset + 1) * tok_rows]
        own_t = own_t + shifted(piece, "seq", offset - span_blocks).astype(jnp.float32)
    own_rows = jnp.swapaxes(own_t, 1, 2)
    chunk = scatter_layers(own_rows)
    kinds, rows, tp_peers, cols = chunk.shape
    d_shared_kv = lax.all_gather(chunk.reshape(kinds, rows, -1), "section", axis=1, tiled=True)
    return (d_queries, d_shared_kv)


def solution(mesh):
    in_specs = (P("section", "seq", "tp"), P("section", "seq", "tp"), P(None, ("seq", "tp"), None))
    out_specs = (P("section", "seq", "tp"), P(None, ("seq", "tp"), None))
    return jax.shard_map(body, mesh=mesh, in_specs=in_specs, out_specs=out_specs, check_vma=False)
```

```python
import functools
import math

import jax
import jax.numpy as jnp
from jax import lax
from jax.experimental import pallas as pl
from jax.experimental.pallas import tpu as pltpu
from jax.sharding import PartitionSpec as P

QH = 64
KVH = 8
HD = 128
WINDOW = 1024


def shifted(value, axis, by):
    peers = lax.axis_size(axis)
    pairs = [(i, i + by) for i in range(peers) if 0 <= i + by < peers]
    return lax.ppermute(value, axis, pairs)


def attn_kernel(bias_ref, q_ref, g_ref, k_ref, v_ref, *rest, scale, hd, per_step, sent_cols, window):
    dq_ref, own_ref, send_ref = rest[-3:]
    k = k_ref[...]
    v = v_ref[...]
    lines = lax.broadcasted_iota(jnp.int32, (q_ref.shape[0], k_ref.shape[0]), 0)
    keys = lax.broadcasted_iota(jnp.int32, (q_ref.shape[0], k_ref.shape[0]), 1)
    allowed = (
        (keys >= lines + 1)
        & (keys <= lines + window)
        & (bias_ref[0] * q_ref.shape[0] - window + keys >= 0)
    )
    bias = jnp.where(allowed, 0.0, -jnp.inf).astype(jnp.float32)
    nt = (((1,), (1,)), ((), ()))
    tn = (((0,), (0,)), ((), ()))
    dk = None
    dv = None
    for part in range(per_step):
        cols = slice(part * hd, (part + 1) * hd)
        q = q_ref[:, cols]
        do = g_ref[:, cols]
        s = lax.dot_general(q, k, nt, preferred_element_type=jnp.float32) * scale + bias
        m = jnp.max(s, axis=1, keepdims=True)
        w = jnp.exp(s - m)
        p = w * (1.0 / jnp.sum(w, axis=1, keepdims=True))
        pb = p.astype(jnp.bfloat16)
        o = jnp.dot(pb, v, preferred_element_type=jnp.float32)
        delta = jnp.sum(do.astype(jnp.float32) * o, axis=1, keepdims=True)
        dp = lax.dot_general(do, v, nt, preferred_element_type=jnp.float32)
        dsb = (p * (dp - delta)).astype(jnp.bfloat16)
        dq = jnp.dot(dsb, k, preferred_element_type=jnp.float32) * scale
        dq_ref[:, cols] = dq.astype(dq_ref.dtype)
        dk_part = lax.dot_general(q, dsb, tn, preferred_element_type=jnp.float32)
        dv_part = lax.dot_general(do, pb, tn, preferred_element_type=jnp.float32)
        dk = dk_part if dk is None else dk + dk_part
        dv = dv_part if dv is None else dv + dv_part

    dk = dk * scale
    own_ref[0] = dk[:, sent_cols:]
    own_ref[1] = dv[:, sent_cols:]
    send_ref[0] = dk[:, :sent_cols].astype(send_ref.dtype)
    send_ref[1] = dv[:, :sent_cols].astype(send_ref.dtype)


def attention_grads(bias, q, g, ext, group, hd, scale, per_step, head0, heads, sent_cols, after=()):
    rows, _ = q.shape
    _, ext_rows, _ = ext.shape
    steps = group // per_step
    assert steps == 1
    width = per_step * hd
    flops = 6 * 2 * rows * ext_rows * hd * heads * group
    return pl.pallas_call(
        functools.partial(attn_kernel, scale=scale, hd=hd, per_step=per_step, sent_cols=sent_cols, window=WINDOW),
        grid=(heads, steps),
        in_specs=[
            pl.BlockSpec(memory_space=pltpu.SMEM),
            pl.BlockSpec((rows, width), lambda h, i: (0, (head0 + h) * steps + i)),
            pl.BlockSpec((rows, width), lambda h, i: (0, (head0 + h) * steps + i)),
            pl.BlockSpec((None, ext_rows, hd), lambda h, i: (0, 0, head0 + h)),
            pl.BlockSpec((None, ext_rows, hd), lambda h, i: (1, 0, head0 + h)),
        ]
        + [pl.BlockSpec(memory_space=pl.ANY) for _ in after],
        out_specs=[
            pl.BlockSpec((rows, width), lambda h, i: (0, h * steps + i)),
            pl.BlockSpec((2, hd, ext_rows - sent_cols), lambda h, i: (0, h, 0)),
            pl.BlockSpec((2, hd, sent_cols), lambda h, i: (0, h, 0)),
        ],
        out_shape=[
            jax.ShapeDtypeStruct((rows, heads * group * hd), jnp.bfloat16),
            jax.ShapeDtypeStruct((2, heads * hd, ext_rows - sent_cols), jnp.float32),
            jax.ShapeDtypeStruct((2, heads * hd, sent_cols), jnp.bfloat16),
        ],
        compiler_params=pltpu.CompilerParams(dimension_semantics=("arbitrary", "arbitrary")),
        cost_estimate=pl.CostEstimate(
            flops=flops,
            transcendentals=rows * ext_rows * heads * group,
            bytes_accessed=(3 * rows * group * 2 + ext_rows * 2 * 6) * hd * heads,
        ),
    )(bias, q, g, ext, ext, *after)


def scatter_layers(own_rows):
    sections = lax.axis_size("section")
    peers = lax.axis_size("tp")
    kinds, rows, cols = own_rows.shape
    pieces = own_rows.reshape(kinds, peers, sections, rows // (peers * sections), cols)
    pieces = jnp.swapaxes(pieces, 1, 2).reshape(kinds, sections * peers, rows // (peers * sections), cols)
    pieces = lax.all_to_all(pieces.astype(jnp.bfloat16), ("section", "tp"), split_axis=1, concat_axis=1)
    pieces = pieces.astype(jnp.float32).reshape(kinds, sections, peers, rows // (peers * sections), cols)
    chunk = pieces[:, 0]
    for other in range(1, sections):
        chunk = chunk + pieces[:, other]
    return jnp.swapaxes(chunk, 1, 2)


def body(queries, upstream, shared_kv):
    local_kv = lax.all_to_all(shared_kv, "tp", split_axis=2, concat_axis=1, tiled=True)
    tok_rows = local_kv.shape[1]
    head_size = HD
    group_size = QH // KVH
    span_blocks = WINDOW // tok_rows
    score_scale = 1.0 / math.sqrt(head_size)
    earlier = [shifted(local_kv, "seq", span_blocks - offset) for offset in range(span_blocks)]
    extended = jnp.concatenate(earlier + [local_kv], axis=1)
    ext_rows = extended.shape[1]
    position = lax.axis_index("seq")
    row_ids = lax.broadcasted_iota(jnp.int32, (tok_rows, ext_rows), 0)
    key_ids = lax.broadcasted_iota(jnp.int32, (tok_rows, ext_rows), 1)
    allowed = (
        (key_ids >= row_ids + 1)
        & (key_ids <= row_ids + WINDOW)
        & (position * tok_rows - WINDOW + key_ids >= 0)
    )
    bias = jnp.reshape(position, (1,)).astype(jnp.int32)
    query_rows = queries.reshape(tok_rows, -1)
    grad_rows = upstream.reshape(tok_rows, -1)
    local_heads = extended.shape[2] // head_size
    d_query_rows, grad_t, sent_t = attention_grads(
        bias, query_rows, grad_rows, extended, group_size, head_size, score_scale, group_size, 0, local_heads,
        span_blocks * tok_rows,
    )
    d_queries = d_query_rows.reshape(queries.shape)
    own_t = grad_t
    for offset in range(span_blocks):
        piece = sent_t[:, :, offset * tok_rows : (offset + 1) * tok_rows]
        own_t = own_t + shifted(piece, "seq", offset - span_blocks).astype(jnp.float32)
    own_rows = jnp.swapaxes(own_t, 1, 2)
    chunk = scatter_layers(own_rows)
    kinds, rows, tp_peers, cols = chunk.shape
    d_shared_kv = lax.all_gather(
        chunk.reshape(kinds, rows, -1).astype(jnp.bfloat16), "section", axis=1, tiled=True
    ).astype(jnp.float32)
    return (d_queries, d_shared_kv)


def solution(mesh):
    in_specs = (P("section", "seq", "tp"), P("section", "seq", "tp"), P(None, ("seq", "tp"), None))
    out_specs = (P("section", "seq", "tp"), P(None, ("seq", "tp"), None))
    return jax.shard_map(body, mesh=mesh, in_specs=in_specs, out_specs=out_specs, check_vma=False)
```
